256 devices in a mesh: dp: 32 (over x, z), tensor: 8 (over y, core).
Axes of the slice: x: 4, y: 4, z: 8, core: 2. Of those that a mesh axis runs over, the one named last changes fastest.
Arguments:
- grads: bfloat16 [32, 8, 1024, 4096], P('dp', 'tensor'), may hold values from -8 to 8
- signs: int32 [8, 4096], P('tensor'), may hold values from 0 to 1
- shifts: int32 [32, 8, 1024], P('dp', 'tensor'), may hold values from 3 to 6
- first: float32 [8, 1024, 4096], P('tensor', 'dp'), may hold values from -1.8 to 1.8
- second: float32 [8, 1024, 4096], P('tensor', 'dp'), may hold values from 0.04 to 0.3
- weights: float32 [8, 1024, 4096], P('tensor', 'dp'), may hold values from -6 to 6
- slots: int32 [32, 8, 8, 16], P('dp', 'tensor'), may hold values from 0 to 31, as said below
- counts: int32 [32, 8, 8], P('dp', 'tensor'), may hold values from 1 to 16, as said below
Outputs:
- new_first: float32 [8, 1024, 4096], P('tensor', 'dp')
- new_second: float32 [8, 1024, 4096], P('tensor', 'dp')
- new_weights: float32 [8, 1024, 4096], P('tensor', 'dp')
- received: bfloat16 [32, 8, 8, 16, 512], P('dp', 'tensor')
The draws below stay inside these ranges and needn't reach their ends.
Inputs may be any that keep to these rules, and one draw needn't show every extreme that they name: The same ids within one list are distinct; slots from the count on are ignored. For each worker row d one owner o has counts[d, t, o] = 16 for every source t.
All inputs are finite; a program needn't handle non-finite values.
Results may differ from the reference program's by a relative error of at most 0.0019.
Values may be sent and summed in bfloat16 or wider, within the bound.
No kernel may reach another device: no remote copies, remote signals or barrier semaphores. Data moves between devices by JAX's collectives and lax.ppermute only.
A program may use at most 128 MiB of HBM per device.

```python
import math
import jax
import jax.numpy as jnp
from jax import lax

HA = 32
HB = 128
H = 4096
BLK_DEV = 32
CAP = 16
WORKERS = 32
OWNERS = 8
TBLK = 1024
PW = 512


def draw_grads(key, part):
    full_shape = (WORKERS, OWNERS, TBLK, H)
    shared = jax.random.normal(jax.random.fold_in(key, 11), (1, OWNERS, TBLK, H), jnp.float32)
    own_part = jax.random.normal(jax.random.fold_in(key, 12), full_shape, jnp.float32)
    values = shared + own_part
    return jnp.clip(values, -8.0, 8.0).astype(jnp.bfloat16)


def draw_slots(key, part):
    total_lists = WORKERS * OWNERS * OWNERS
    list_keys = jax.random.split(jax.random.fold_in(key, 21), total_lists)
    orders = jax.vmap(lambda one_key: jax.random.permutation(one_key, BLK_DEV))(list_keys)
    return orders[:, :CAP].reshape(WORKERS, OWNERS, OWNERS, CAP).astype(jnp.int32)


def draw_counts(key, part):
    base_counts = jax.random.randint(jax.random.fold_in(key, 31), (WORKERS, OWNERS, OWNERS), 1, CAP + 1)
    full_owner = jax.random.randint(jax.random.fold_in(key, 32), (WORKERS,), 0, OWNERS)
    is_full = jnp.arange(OWNERS, dtype=jnp.int32)[None, None, :] == full_owner[:, None, None]
    return jnp.where(is_full, CAP, base_counts).astype(jnp.int32)


def touch_ends(drawn, stream_key, least, top_value):
    dims = drawn.shape
    place = [jax.random.randint(jax.random.fold_in(stream_key, axis), (), 0, dims[axis]) for axis in range(len(dims))]
    drawn = drawn.at[tuple(place)].set(least)
    longest = dims.index(max(dims))
    place[longest] = (place[longest] + 1) % dims[longest]
    return drawn.at[tuple(place)].set(top_value)


def shard_levels(own_key, shape, shards, smallest, high):
    def one(position, shards_of):
        steps = jax.random.uniform(jax.random.fold_in(jax.random.fold_in(own_key, 6), position), (shards_of,), jnp.float32, smallest / len(shards), high / len(shards))
        return jnp.repeat(jnp.exp(steps), shape[position] // shards_of).reshape((-1,) + (1,) * (len(shape) - position - 1))

    loudness = one(*shards[0])
    for cut in shards[1:]:
        loudness = loudness * one(*cut)
    return loudness


def bell_draw(rng, extent, scale, bound, cuts=(), held_as=jnp.bfloat16):
    entries = jax.random.normal(rng, extent, jnp.float32) * scale
    if len(cuts) > 0:
        entries = shard_levels(rng, extent, cuts, -0.22, 0.18) * entries
    return jnp.clip(entries, min=-bound, max=bound).astype(held_as)


def setup_inputs(seed: int = 0) -> dict:
    key_of = jax.random.split(jax.random.key(seed), 9)
    grads = draw_grads(jax.random.fold_in(key_of[8], 71), 0)
    signs = touch_ends(jax.random.randint(key_of[1], (OWNERS, H), 0, 2), jax.random.fold_in(key_of[1], 1), 0, 1).astype(jnp.int32)
    shifts = touch_ends(jax.random.randint(key_of[2], (WORKERS, OWNERS, TBLK), 3, 7), jax.random.fold_in(key_of[2], 1), 3, 6).astype(jnp.int32)
    first = bell_draw(key_of[3], (OWNERS, TBLK, H), 0.3, 1.8, ((0, 8), (1, 32)), jnp.float32)
    second = jnp.clip(jnp.exp(math.log(0.3) - 2.014903 * jax.random.uniform(key_of[4], (OWNERS, TBLK, H), jnp.float32) ** shard_levels(key_of[4], (OWNERS, TBLK, H), ((0, 8), (1, 32)), -0.2, 0.2)), 0.04, 0.3)
    weights = bell_draw(key_of[5], (OWNERS, TBLK, H), 1.0, 6.0, ((0, 8), (1, 32)), jnp.float32)
    slots = draw_slots(jax.random.fold_in(key_of[8], 71), 0)
    counts = draw_counts(jax.random.fold_in(key_of[8], 71), 0)
    return {"grads": grads, "signs": signs, "shifts": shifts, "first": first, "second": second, "weights": weights, "slots": slots, "counts": counts}


first_keep = 0.9
first_take = 0.1
second_keep = 0.95
second_take = 0.05
first_fix = 1.0 - 0.9 ** 10
second_fix = 1.0 - 0.95 ** 10
adam_eps = 1e-08
learn_rate = 0.2

def walsh_table(table_order):
    positions = jnp.arange(table_order, dtype=jnp.int32)
    common_bits = jnp.bitwise_and(positions[:, None], positions[None, :])
    parity_sum = jnp.zeros((table_order, table_order), jnp.int32)
    for bit_level in range(max(table_order.bit_length() - 1, 1)):
        parity_sum = parity_sum + jnp.bitwise_and(jnp.right_shift(common_bits, bit_level), 1)
    return (1 - 2 * jnp.bitwise_and(parity_sum, 1)).astype(jnp.float32)

def rotate(flat_rows):
    count_rows = flat_rows.shape[0]
    cube_rows = flat_rows.reshape(count_rows, HA, HB)
    cube_rows = jnp.einsum('rab,bc->rac', cube_rows, walsh_table(HB), precision=lax.Precision.HIGHEST)
    cube_rows = jnp.einsum('ka,rac->rkc', walsh_table(HA), cube_rows, precision=lax.Precision.HIGHEST)
    return cube_rows.reshape(count_rows, HA * HB) / math.sqrt(HA * HB)

def half_power(shift_vals):
    unit_scale = jnp.ones(shift_vals.shape, jnp.float32)
    factor = 0.5
    for bit_level in range(5):
        chosen = jnp.bitwise_and(jnp.right_shift(shift_vals, bit_level), 1) == 1
        unit_scale = unit_scale * jnp.where(chosen, factor, 1.0).astype(jnp.float32)
        factor = factor * factor
    return unit_scale

def reference(grads, signs, shifts, first, second, weights, slots, counts):
    sign_vec = (2 * signs - 1).astype(jnp.float32)

    def add_worker(summed, inputs):
        worker_grad, worker_shift = inputs
        flipped = worker_grad.astype(jnp.float32) * sign_vec[:, None, :]
        rotated = rotate(flipped.reshape(-1, H)).reshape(flipped.shape)
        unit_scale = half_power(worker_shift)[..., None]
        coded = jnp.clip(rotated / unit_scale, -127.0, 127.0).astype(jnp.bfloat16)
        return (summed + coded.astype(jnp.float32) * unit_scale, None)
    summed, _ = lax.scan(add_worker, jnp.zeros(first.shape, jnp.float32), (grads, shifts))
    mean_grad = summed / WORKERS
    new_first = first_keep * first + first_take * mean_grad
    new_second = second_keep * second + second_take * mean_grad * mean_grad
    step_dir = new_first / first_fix / (jnp.sqrt(new_second / second_fix) + adam_eps)
    weight_step = rotate(step_dir.reshape(-1, H)).reshape(step_dir.shape) * sign_vec[:, None, :]
    new_weights = weights - learn_rate * weight_step
    pieces = new_weights.astype(jnp.bfloat16).reshape(OWNERS, WORKERS, BLK_DEV, OWNERS, PW)
    worker_axis = jnp.arange(WORKERS, dtype=jnp.int32)[:, None, None, None]
    source_axis = jnp.arange(OWNERS, dtype=jnp.int32)[None, :, None, None]
    owner_axis = jnp.arange(OWNERS, dtype=jnp.int32)[None, None, :, None]
    picked = pieces[source_axis, worker_axis, slots, owner_axis]
    live_slots = jnp.arange(CAP, dtype=jnp.int32)[None, None, None, :] < counts[..., None]
    picked = jnp.where(live_slots[..., None], picked, jnp.zeros((), jnp.bfloat16))
    received = jnp.transpose(picked, (0, 2, 1, 3, 4))
    return (new_first, new_second, new_weights, received)
```

```python
import math

import jax
import jax.numpy as jnp
from jax import lax
from jax.experimental import pallas as pl
from jax.experimental.pallas import tpu as pltpu
from jax.sharding import PartitionSpec as P

HA = 32
HB = 128
ROW_TILE = 256


first_keep = 0.9
first_take = 0.1
second_keep = 0.95
second_take = 0.05
first_fix = 1.0 - 0.9**10
second_fix = 1.0 - 0.95**10
adam_eps = 1e-08
learn_rate = 0.2


def walsh_table(table_order):
    positions = jnp.arange(table_order, dtype=jnp.int32)
    common_bits = jnp.bitwise_and(positions[:, None], positions[None, :])
    parity_sum = jnp.zeros((table_order, table_order), jnp.int32)
    for bit_level in range(max(table_order.bit_length() - 1, 1)):
        parity_sum = parity_sum + jnp.bitwise_and(jnp.right_shift(common_bits, bit_level), 1)
    return (1 - 2 * jnp.bitwise_and(parity_sum, 1)).astype(jnp.float32)


def rotate(flat_rows):
    count_rows = flat_rows.shape[0]
    cube_rows = flat_rows.reshape(count_rows, HA, HB)
    cube_rows = jnp.einsum(
        "rab,bc->rac", cube_rows, walsh_table(HB), precision=lax.Precision.HIGHEST
    )
    cube_rows = jnp.einsum(
        "ka,rac->rkc", walsh_table(HA), cube_rows, precision=lax.Precision.HIGHEST
    )
    return cube_rows.reshape(count_rows, HA * HB) / math.sqrt(HA * HB)


def half_power(shift_vals):
    unit_scale = jnp.ones(shift_vals.shape, jnp.float32)
    factor = 0.5
    for bit_level in range(5):
        chosen = jnp.bitwise_and(jnp.right_shift(shift_vals, bit_level), 1) == 1
        unit_scale = unit_scale * jnp.where(chosen, factor, 1.0).astype(jnp.float32)
        factor = factor * factor
    return unit_scale


def butterfly(blocks):
    blocks = list(blocks)
    span = 1
    while span < len(blocks):
        for start in range(0, len(blocks), 2 * span):
            for j in range(start, start + span):
                u, v = blocks[j], blocks[j + span]
                blocks[j], blocks[j + span] = u + v, u - v
        span *= 2
    return blocks


def code_kernel(x_ref, w_ref, up_ref, dn_ref, o_ref, y_ref):
    for a in range(HA):
        cols = slice(a * HB, (a + 1) * HB)
        y_ref[:, cols] = jnp.dot(x_ref[:, cols], w_ref[a], preferred_element_type=jnp.float32)

    def row_group(g, carry):
        rows = pl.ds(pl.multiple_of(g * 8, 8), 8)
        blocks = butterfly([y_ref[rows, a * HB:(a + 1) * HB] for a in range(HA)])
        up = up_ref[rows, :]
        dn = dn_ref[rows, :]
        for a in range(HA):
            coded = jnp.clip(blocks[a] * up, -127.0, 127.0).astype(jnp.bfloat16)
            o_ref[rows, a * HB:(a + 1) * HB] = (coded.astype(jnp.float32) * dn).astype(o_ref.dtype)
        return carry

    lax.fori_loop(0, x_ref.shape[0] // 8, row_group, 0)


def decoded_terms(grad_rows, signed_walsh, up_scale, down_scale):
    rows, width = grad_rows.shape
    return pl.pallas_call(
        code_kernel,
        grid=(rows // ROW_TILE,),
        in_specs=[
            pl.BlockSpec((ROW_TILE, width), lambda i: (i, 0)),
            pl.BlockSpec((HA, HB, HB), lambda i: (0, 0, 0)),
            pl.BlockSpec((ROW_TILE, 1), lambda i: (i, 0)),
            pl.BlockSpec((ROW_TILE, 1), lambda i: (i, 0)),
        ],
        out_specs=pl.BlockSpec((ROW_TILE, width), lambda i: (i, 0)),
        out_shape=jax.ShapeDtypeStruct((rows, width), jnp.bfloat16),
        scratch_shapes=[pltpu.VMEM((ROW_TILE, width), jnp.float32)],
        cost_estimate=pl.CostEstimate(
            flops=2 * rows * width * HB + 8 * rows * width,
            transcendentals=0,
            bytes_accessed=rows * width * 4,
        ),
    )(grad_rows, signed_walsh, up_scale, down_scale)


def select_pieces(slab_view, slot_lists, used_counts):
    gathered = jnp.take_along_axis(slab_view, slot_lists[:, :, None], axis=1)
    live_slots = lax.broadcasted_iota(jnp.int32, slot_lists.shape, 1) < used_counts[:, None]
    return jnp.where(live_slots[:, :, None], gathered, jnp.zeros((), jnp.bfloat16))


def per_device(grads, signs, shifts, first, second, weights, slots, counts):
    sign_vec = (2 * signs[0] - 1).astype(jnp.float32)
    grad_rows = grads[0, 0]
    shift_rows = shifts[0, 0]
    blocks = first.shape[1]
    signed_walsh = (sign_vec.reshape(HA, HB, 1) * walsh_table(HB)[None]).astype(jnp.bfloat16)
    unit_scale = half_power(shift_rows)[:, None]
    up_scale = (1.0 / unit_scale) / math.sqrt(HA * HB)
    terms = decoded_terms(grad_rows, signed_walsh, up_scale, unit_scale)
    workers = lax.axis_size("dp")
    arrived_terms = lax.all_to_all(terms, "dp", split_axis=0, concat_axis=0, tiled=True)
    summed = arrived_terms.reshape(workers, blocks, -1).astype(jnp.float32).sum(0)
    mean_grad = summed / workers
    new_first = first_keep * first[0] + first_take * mean_grad
    new_second = second_keep * second[0] + second_take * mean_grad * mean_grad
    step_dir = new_first / first_fix / (jnp.sqrt(new_second / second_fix) + adam_eps)
    weight_step = rotate(step_dir) * sign_vec[None, :]
    new_weights = weights[0] - learn_rate * weight_step
    owners = lax.axis_size("tensor")
    piece_width = new_weights.shape[1] // owners
    narrow = new_weights.astype(jnp.bfloat16).reshape(blocks, owners, piece_width)
    slab_view = jnp.transpose(narrow, (1, 0, 2))
    slot_lists = slots[0, 0]
    used_counts = counts[0, 0]
    chosen_pieces = select_pieces(slab_view, slot_lists, used_counts)
    arrived = lax.all_to_all(chosen_pieces, "tensor", split_axis=0, concat_axis=0, tiled=True)
    return (new_first[None], new_second[None], new_weights[None], arrived[None, None])


def solution(mesh):
    return jax.shard_map(
        per_device,
        mesh=mesh,
        in_specs=(
            P("dp", "tensor", None, None),
            P("tensor", None),
            P("dp", "tensor", None),
            P("tensor", "dp", None),
            P("tensor", "dp", None),
            P("tensor", "dp", None),
            P("dp", "tensor", None, None),
            P("dp", "tensor", None),
        ),
        out_specs=(
            P("tensor", "dp", None),
            P("tensor", "dp", None),
            P("tensor", "dp", None),
            P("dp", "tensor", None, None, None),
        ),
        check_vma=False,
    )
```

```python
import math

import jax
import jax.numpy as jnp
from jax import lax
from jax.experimental import pallas as pl
from jax.experimental.pallas import tpu as pltpu
from jax.sharding import Mesh
from jax.sharding import PartitionSpec as P

HA = 32
HB = 128
ROW_TILE = 256
X_CHIPS = 4
WORKERS = ("wx", "wz")


first_keep = 0.9
first_take = 0.1
second_keep = 0.95
second_take = 0.05
first_fix = 1.0 - 0.9**10
second_fix = 1.0 - 0.95**10
adam_eps = 1e-08
learn_rate = 0.2


def walsh_table(table_order):
    positions = jnp.arange(table_order, dtype=jnp.int32)
    common_bits = jnp.bitwise_and(positions[:, None], positions[None, :])
    parity_sum = jnp.zeros((table_order, table_order), jnp.int32)
    for bit_level in range(max(table_order.bit_length() - 1, 1)):
        parity_sum = parity_sum + jnp.bitwise_and(jnp.right_shift(common_bits, bit_level), 1)
    return (1 - 2 * jnp.bitwise_and(parity_sum, 1)).astype(jnp.float32)


def rotate(flat_rows):
    count_rows = flat_rows.shape[0]
    cube_rows = flat_rows.reshape(count_rows, HA, HB)
    cube_rows = jnp.einsum(
        "rab,bc->rac", cube_rows, walsh_table(HB), precision=lax.Precision.HIGHEST
    )
    cube_rows = jnp.einsum(
        "ka,rac->rkc", walsh_table(HA), cube_rows, precision=lax.Precision.HIGHEST
    )
    return cube_rows.reshape(count_rows, HA * HB) / math.sqrt(HA * HB)


def half_power(shift_vals):
    unit_scale = jnp.ones(shift_vals.shape, jnp.float32)
    factor = 0.5
    for bit_level in range(5):
        chosen = jnp.bitwise_and(jnp.right_shift(shift_vals, bit_level), 1) == 1
        unit_scale = unit_scale * jnp.where(chosen, factor, 1.0).astype(jnp.float32)
        factor = factor * factor
    return unit_scale


def butterfly(blocks):
    blocks = list(blocks)
    span = 1
    while span < len(blocks):
        for start in range(0, len(blocks), 2 * span):
            for j in range(start, start + span):
                u, v = blocks[j], blocks[j + span]
                blocks[j], blocks[j + span] = u + v, u - v
        span *= 2
    return blocks


def code_kernel(x_ref, w_ref, up_ref, dn_ref, o_ref, y_ref):
    for a in range(HA):
        cols = slice(a * HB, (a + 1) * HB)
        y_ref[:, cols] = jnp.dot(x_ref[:, cols], w_ref[a], preferred_element_type=jnp.float32)

    def row_group(g, carry):
        rows = pl.ds(pl.multiple_of(g * 8, 8), 8)
        blocks = butterfly([y_ref[rows, a * HB:(a + 1) * HB] for a in range(HA)])
        up = up_ref[rows, :]
        dn = dn_ref[rows, :]
        for a in range(HA):
            coded = jnp.clip(blocks[a] * up, -127.0, 127.0).astype(jnp.bfloat16)
            o_ref[rows, a * HB:(a + 1) * HB] = (coded.astype(jnp.float32) * dn).astype(o_ref.dtype)
        return carry

    lax.fori_loop(0, x_ref.shape[0] // 8, row_group, 0)


def decoded_terms(grad_rows, signed_walsh, up_scale, down_scale):
    rows, width = grad_rows.shape
    return pl.pallas_call(
        code_kernel,
        grid=(rows // ROW_TILE,),
        in_specs=[
            pl.BlockSpec((ROW_TILE, width), lambda i: (i, 0)),
            pl.BlockSpec((HA, HB, HB), lambda i: (0, 0, 0)),
            pl.BlockSpec((ROW_TILE, 1), lambda i: (i, 0)),
            pl.BlockSpec((ROW_TILE, 1), lambda i: (i, 0)),
        ],
        out_specs=pl.BlockSpec((ROW_TILE, width), lambda i: (i, 0)),
        out_shape=jax.ShapeDtypeStruct((rows, width), jnp.bfloat16),
        scratch_shapes=[pltpu.VMEM((ROW_TILE, width), jnp.float32)],
        cost_estimate=pl.CostEstimate(
            flops=2 * rows * width * HB + 8 * rows * width,
            transcendentals=0,
            bytes_accessed=rows * width * 4,
        ),
    )(grad_rows, signed_walsh, up_scale, down_scale)


def select_pieces(slab_view, slot_lists, used_counts):
    gathered = jnp.take_along_axis(slab_view, slot_lists[:, :, None], axis=1)
    live_slots = lax.broadcasted_iota(jnp.int32, slot_lists.shape, 1) < used_counts[:, None]
    return jnp.where(live_slots[:, :, None], gathered, jnp.zeros((), jnp.bfloat16))


def per_device(grads, signs, shifts, first, second, weights, slots, counts):
    sign_vec = (2 * signs[0] - 1).astype(jnp.float32)
    grad_rows = grads[0, 0]
    shift_rows = shifts[0, 0]
    blocks = first.shape[1]
    signed_walsh = (sign_vec.reshape(HA, HB, 1) * walsh_table(HB)[None]).astype(jnp.bfloat16)
    unit_scale = half_power(shift_rows)[:, None]
    up_scale = (1.0 / unit_scale) / math.sqrt(HA * HB)
    terms = decoded_terms(grad_rows, signed_walsh, up_scale, unit_scale)
    x_size = lax.axis_size("wx")
    workers = x_size * lax.axis_size("wz")
    arrived_terms = lax.all_to_all(terms, "wx", split_axis=0, concat_axis=0, tiled=True)
    partial = arrived_terms.reshape(x_size, grad_rows.shape[0] // x_size, -1).astype(jnp.float32).sum(0)
    summed = lax.psum_scatter(partial, "wz", scatter_dimension=0, tiled=True)
    mean_grad = summed / workers
    new_first = first_keep * first[0] + first_take * mean_grad
    new_second = second_keep * second[0] + second_take * mean_grad * mean_grad
    step_dir = new_first / first_fix / (jnp.sqrt(new_second / second_fix) + adam_eps)
    weight_step = rotate(step_dir) * sign_vec[None, :]
    new_weights = weights[0] - learn_rate * weight_step
    owners = lax.axis_size("tensor")
    piece_width = new_weights.shape[1] // owners
    narrow = new_weights.astype(jnp.bfloat16).reshape(blocks, owners, piece_width)
    slab_view = jnp.transpose(narrow, (1, 0, 2))
    slot_lists = slots[0, 0]
    used_counts = counts[0, 0]
    chosen_pieces = select_pieces(slab_view, slot_lists, used_counts)
    arrived = lax.all_to_all(chosen_pieces, "tensor", split_axis=0, concat_axis=0, tiled=True)
    return (new_first[None], new_second[None], new_weights[None], arrived[None, None])


def solution(mesh):
    dp_size, tensor_size = mesh.devices.shape
    split_mesh = Mesh(
        mesh.devices.reshape(X_CHIPS, dp_size // X_CHIPS, tensor_size), WORKERS + ("tensor",)
    )
    return jax.shard_map(
        per_device,
        mesh=split_mesh,
        in_specs=(
            P(WORKERS, "tensor", None, None),
            P("tensor", None),
            P(WORKERS, "tensor", None),
            P("tensor", WORKERS, None),
            P("tensor", WORKERS, None),
            P("tensor", WORKERS, None),
            P(WORKERS, "tensor", None, None),
            P(WORKERS, "tensor", None),
        ),
        out_specs=(
            P("tensor", WORKERS, None),
            P("tensor", WORKERS, None),
            P("tensor", WORKERS, None),
            P(WORKERS, "tensor", None, None, None),
        ),
        check_vma=False,
    )
```

```python
import math

import jax
import jax.numpy as jnp
from jax import lax
from jax.experimental import pallas as pl
from jax.experimental.pallas import tpu as pltpu
from jax.sharding import Mesh
from jax.sharding import PartitionSpec as P

HA = 32
HB = 128
ROW_TILE = 256
X_CHIPS = 4
PARTS = 2
WORKERS = ("wx", "wz")


first_keep = 0.9
first_take = 0.1
second_keep = 0.95
second_take = 0.05
first_fix = 1.0 - 0.9**10
second_fix = 1.0 - 0.95**10
adam_eps = 1e-08
learn_rate = 0.2


def walsh_table(table_order):
    positions = jnp.arange(table_order, dtype=jnp.int32)
    common_bits = jnp.bitwise_and(positions[:, None], positions[None, :])
    parity_sum = jnp.zeros((table_order, table_order), jnp.int32)
    for bit_level in range(max(table_order.bit_length() - 1, 1)):
        parity_sum = parity_sum + jnp.bitwise_and(jnp.right_shift(common_bits, bit_level), 1)
    return (1 - 2 * jnp.bitwise_and(parity_sum, 1)).astype(jnp.float32)


def rotate(flat_rows):
    count_rows = flat_rows.shape[0]
    cube_rows = flat_rows.reshape(count_rows, HA, HB)
    cube_rows = jnp.einsum(
        "rab,bc->rac", cube_rows, walsh_table(HB), precision=lax.Precision.HIGHEST
    )
    cube_rows = jnp.einsum(
        "ka,rac->rkc", walsh_table(HA), cube_rows, precision=lax.Precision.HIGHEST
    )
    return cube_rows.reshape(count_rows, HA * HB) / math.sqrt(HA * HB)


def half_power(shift_vals):
    unit_scale = jnp.ones(shift_vals.shape, jnp.float32)
    factor = 0.5
    for bit_level in range(5):
        chosen = jnp.bitwise_and(jnp.right_shift(shift_vals, bit_level), 1) == 1
        unit_scale = unit_scale * jnp.where(chosen, factor, 1.0).astype(jnp.float32)
        factor = factor * factor
    return unit_scale


def butterfly(blocks):
    blocks = list(blocks)
    span = 1
    while span < len(blocks):
        for start in range(0, len(blocks), 2 * span):
            for j in range(start, start + span):
                u, v = blocks[j], blocks[j + span]
                blocks[j], blocks[j + span] = u + v, u - v
        span *= 2
    return blocks


def code_kernel(x_ref, w_ref, up_ref, dn_ref, o_ref, y_ref):
    groups, group_rows, _ = x_ref.shape
    for a in range(HA):
        cols = slice(a * HB, (a + 1) * HB)
        lhs = x_ref[:, :, cols].reshape(groups * group_rows, HB)
        y_ref[:, cols] = jnp.dot(lhs, w_ref[a], preferred_element_type=jnp.float32)

    def row_group(g, carry):
        rows = pl.ds(pl.multiple_of(g * 8, 8), 8)
        dest = g // (group_rows // 8)
        within = pl.ds(pl.multiple_of((g % (group_rows // 8)) * 8, 8), 8)
        blocks = butterfly([y_ref[rows, a * HB:(a + 1) * HB] for a in range(HA)])
        up = up_ref[dest, within, :]
        dn = dn_ref[dest, within, :]
        for a in range(HA):
            coded = jnp.clip(blocks[a] * up, -127.0, 127.0).astype(jnp.bfloat16)
            o_ref[rows, a * HB:(a + 1) * HB] = (coded.astype(jnp.float32) * dn).astype(o_ref.dtype)
        return carry

    lax.fori_loop(0, groups * group_rows // 8, row_group, 0)


def decoded_terms(grad_groups, signed_walsh, up_scale, down_scale, part, x_size):
    dests, _, part_rows, width = grad_groups.shape
    per_x = dests // x_size
    tile = lambda i: (i, part, 0, 0)
    return pl.pallas_call(
        code_kernel,
        grid=(x_size,),
        in_specs=[
            pl.BlockSpec((per_x, None, part_rows, width), tile),
            pl.BlockSpec((HA, HB, HB), lambda i: (0, 0, 0)),
            pl.BlockSpec((per_x, None, part_rows, 1), tile),
            pl.BlockSpec((per_x, None, part_rows, 1), tile),
        ],
        out_specs=pl.BlockSpec((None, per_x * part_rows, width), lambda i: (i, 0, 0)),
        out_shape=jax.ShapeDtypeStruct((x_size, per_x * part_rows, width), jnp.bfloat16),
        scratch_shapes=[pltpu.VMEM((per_x * part_rows, width), jnp.float32)],
        cost_estimate=pl.CostEstimate(
            flops=2 * dests * part_rows * width * HB + 8 * dests * part_rows * width,
            transcendentals=0,
            bytes_accessed=dests * part_rows * width * 4,
        ),
    )(grad_groups, signed_walsh, up_scale, down_scale)


def select_pieces(slab_view, slot_lists, used_counts):
    gathered = jnp.take_along_axis(slab_view, slot_lists[:, :, None], axis=1)
    live_slots = lax.broadcasted_iota(jnp.int32, slot_lists.shape, 1) < used_counts[:, None]
    return jnp.where(live_slots[:, :, None], gathered, jnp.zeros((), jnp.bfloat16))


def per_device(grads, signs, shifts, first, second, weights, slots, counts):
    sign_vec = (2 * signs[0] - 1).astype(jnp.float32)
    grad_rows = grads[0, 0]
    shift_rows = shifts[0, 0]
    blocks = first.shape[1]
    signed_walsh = (sign_vec.reshape(HA, HB, 1) * walsh_table(HB)[None]).astype(jnp.bfloat16)
    unit_scale = half_power(shift_rows)[:, None]
    up_scale = (1.0 / unit_scale) / math.sqrt(HA * HB)
    x_size = lax.axis_size("wx")
    dests = x_size * lax.axis_size("wz")
    workers = dests
    part_rows = blocks // PARTS
    as_groups = lambda rows: rows.reshape(dests, PARTS, part_rows, rows.shape[-1])
    grad_groups = as_groups(grad_rows)
    up_groups, down_groups = as_groups(up_scale), as_groups(unit_scale)
    pieces = []
    for part in range(PARTS):
        terms = decoded_terms(grad_groups, signed_walsh, up_groups, down_groups, part, x_size)
        arrived_terms = lax.all_to_all(terms, "wx", split_axis=0, concat_axis=0, tiled=True)
        partial = arrived_terms.astype(jnp.float32).sum(0)
        pieces.append(lax.psum_scatter(partial, "wz", scatter_dimension=0, tiled=True))
    summed = jnp.concatenate(pieces, 0)
    mean_grad = summed / workers
    new_first = first_keep * first[0] + first_take * mean_grad
    new_second = second_keep * second[0] + second_take * mean_grad * mean_grad
    step_dir = new_first / first_fix / (jnp.sqrt(new_second / second_fix) + adam_eps)
    weight_step = rotate(step_dir) * sign_vec[None, :]
    new_weights = weights[0] - learn_rate * weight_step
    owners = lax.axis_size("tensor")
    piece_width = new_weights.shape[1] // owners
    narrow = new_weights.astype(jnp.bfloat16).reshape(blocks, owners, piece_width)
    slab_view = jnp.transpose(narrow, (1, 0, 2))
    slot_lists = slots[0, 0]
    used_counts = counts[0, 0]
    chosen_pieces = select_pieces(slab_view, slot_lists, used_counts)
    arrived = lax.all_to_all(chosen_pieces, "tensor", split_axis=0, concat_axis=0, tiled=True)
    return (new_first[None], new_second[None], new_weights[None], arrived[None, None])


def solution(mesh):
    dp_size, tensor_size = mesh.devices.shape
    split_mesh = Mesh(
        mesh.devices.reshape(X_CHIPS, dp_size // X_CHIPS, tensor_size), WORKERS + ("tensor",)
    )
    return jax.shard_map(
        per_device,
        mesh=split_mesh,
        in_specs=(
            P(WORKERS, "tensor", None, None),
            P("tensor", None),
            P(WORKERS, "tensor", None),
            P("tensor", WORKERS, None),
            P("tensor", WORKERS, None),
            P("tensor", WORKERS, None),
            P(WORKERS, "tensor", None, None),
            P(WORKERS, "tensor", None),
        ),
        out_specs=(
            P("tensor", WORKERS, None),
            P("tensor", WORKERS, None),
            P("tensor", WORKERS, None),
            P(WORKERS, "tensor", None, None, None),
        ),
        check_vma=False,
    )
```

```python
import math

import jax
import jax.numpy as jnp
from jax import lax
from jax.experimental import pallas as pl
from jax.experimental.pallas import tpu as pltpu
from jax.sharding import Mesh
from jax.sharding import PartitionSpec as P

HA = 32
HB = 128
ROW_TILE = 256
X_CHIPS = 4
PARTS = 2
WORKERS = ("wx", "wz")


first_keep = 0.9
first_take = 0.1
second_keep = 0.95
second_take = 0.05
first_fix = 1.0 - 0.9**10
second_fix = 1.0 - 0.95**10
adam_eps = 1e-08
learn_rate = 0.2


def walsh_table(table_order):
    positions = jnp.arange(table_order, dtype=jnp.int32)
    common_bits = jnp.bitwise_and(positions[:, None], positions[None, :])
    parity_sum = jnp.zeros((table_order, table_order), jnp.int32)
    for bit_level in range(max(table_order.bit_length() - 1, 1)):
        parity_sum = parity_sum + jnp.bitwise_and(jnp.right_shift(common_bits, bit_level), 1)
    return (1 - 2 * jnp.bitwise_and(parity_sum, 1)).astype(jnp.float32)


def rotate(flat_rows):
    count_rows = flat_rows.shape[0]
    cube_rows = flat_rows.reshape(count_rows, HA, HB)
    cube_rows = jnp.einsum(
        "rab,bc->rac", cube_rows, walsh_table(HB), precision=lax.Precision.HIGHEST
    )
    cube_rows = jnp.einsum(
        "ka,rac->rkc", walsh_table(HA), cube_rows, precision=lax.Precision.HIGHEST
    )
    return cube_rows.reshape(count_rows, HA * HB) / math.sqrt(HA * HB)


def half_power(shift_vals):
    unit_scale = jnp.ones(shift_vals.shape, jnp.float32)
    factor = 0.5
    for bit_level in range(5):
        chosen = jnp.bitwise_and(jnp.right_shift(shift_vals, bit_level), 1) == 1
        unit_scale = unit_scale * jnp.where(chosen, factor, 1.0).astype(jnp.float32)
        factor = factor * factor
    return unit_scale


def butterfly(blocks):
    blocks = list(blocks)
    span = 1
    while span < len(blocks):
        for start in range(0, len(blocks), 2 * span):
            for j in range(start, start + span):
                u, v = blocks[j], blocks[j + span]
                blocks[j], blocks[j + span] = u + v, u - v
        span *= 2
    return blocks


def code_kernel(x_ref, w_ref, up_ref, dn_ref, o_ref, y_ref):
    groups, group_rows, _ = x_ref.shape
    for a in range(HA):
        cols = slice(a * HB, (a + 1) * HB)
        lhs = x_ref[:, :, cols].reshape(groups * group_rows, HB)
        y_ref[:, cols] = jnp.dot(lhs, w_ref[a], preferred_element_type=jnp.float32)

    def row_group(g, carry):
        rows = pl.ds(pl.multiple_of(g * 8, 8), 8)
        dest = g // (group_rows // 8)
        within = pl.ds(pl.multiple_of((g % (group_rows // 8)) * 8, 8), 8)
        blocks = butterfly([y_ref[rows, a * HB:(a + 1) * HB] for a in range(HA)])
        up = up_ref[dest, within, :]
        dn = dn_ref[dest, within, :]
        for a in range(HA):
            coded = jnp.clip(blocks[a] * up, -127.0, 127.0).astype(jnp.bfloat16)
            o_ref[rows, a * HB:(a + 1) * HB] = (coded.astype(jnp.float32) * dn).astype(o_ref.dtype)
        return carry

    lax.fori_loop(0, groups * group_rows // 8, row_group, 0)


def decoded_terms(grad_groups, signed_walsh, up_scale, down_scale, part, x_size):
    dests, _, part_rows, width = grad_groups.shape
    per_x = dests // x_size
    tile = lambda i: (i, part, 0, 0)
    return pl.pallas_call(
        code_kernel,
        grid=(x_size,),
        in_specs=[
            pl.BlockSpec((per_x, None, part_rows, width), tile),
            pl.BlockSpec((HA, HB, HB), lambda i: (0, 0, 0)),
            pl.BlockSpec((per_x, None, part_rows, 1), tile),
            pl.BlockSpec((per_x, None, part_rows, 1), tile),
        ],
        out_specs=pl.BlockSpec((None, per_x * part_rows, width), lambda i: (i, 0, 0)),
        out_shape=jax.ShapeDtypeStruct((x_size, per_x * part_rows, width), jnp.bfloat16),
        scratch_shapes=[pltpu.VMEM((per_x * part_rows, width), jnp.float32)],
        cost_estimate=pl.CostEstimate(
            flops=2 * dests * part_rows * width * HB + 8 * dests * part_rows * width,
            transcendentals=0,
            bytes_accessed=dests * part_rows * width * 4,
        ),
    )(grad_groups, signed_walsh, up_scale, down_scale)


def send_along_x(terms, x_size):
    my_x = lax.axis_index("wx")
    arrived = [lax.dynamic_index_in_dim(terms, my_x, 0, keepdims=False)]
    for step in range(1, x_size):
        outgoing = lax.dynamic_index_in_dim(terms, (my_x + step) % x_size, 0, keepdims=False)
        pairs = [(i, (i + step) % x_size) for i in range(x_size)]
        arrived.append(lax.ppermute(outgoing, "wx", pairs))
    return arrived


def sum_arrived(arrived):
    partial = arrived[0].astype(jnp.float32)
    for piece in arrived[1:]:
        partial = partial + piece.astype(jnp.float32)
    return partial


def select_pieces(slab_view, slot_lists, used_counts):
    gathered = jnp.take_along_axis(slab_view, slot_lists[:, :, None], axis=1)
    live_slots = lax.broadcasted_iota(jnp.int32, slot_lists.shape, 1) < used_counts[:, None]
    return jnp.where(live_slots[:, :, None], gathered, jnp.zeros((), jnp.bfloat16))


def per_device(grads, signs, shifts, first, second, weights, slots, counts):
    sign_vec = (2 * signs[0] - 1).astype(jnp.float32)
    grad_rows = grads[0, 0]
    shift_rows = shifts[0, 0]
    blocks = first.shape[1]
    signed_walsh = (sign_vec.reshape(HA, HB, 1) * walsh_table(HB)[None]).astype(jnp.bfloat16)
    unit_scale = half_power(shift_rows)[:, None]
    up_scale = (1.0 / unit_scale) / math.sqrt(HA * HB)
    x_size = lax.axis_size("wx")
    dests = x_size * lax.axis_size("wz")
    workers = dests
    part_rows = blocks // PARTS
    as_groups = lambda rows: rows.reshape(dests, PARTS, part_rows, rows.shape[-1])
    grad_groups = as_groups(grad_rows)
    up_groups, down_groups = as_groups(up_scale), as_groups(unit_scale)
    pieces = []
    terms = decoded_terms(grad_groups, signed_walsh, up_groups, down_groups, 0, x_size)
    arrived = send_along_x(terms, x_size)
    for part in range(1, PARTS + 1):
        if part < PARTS:
            terms = decoded_terms(grad_groups, signed_walsh, up_groups, down_groups, part, x_size)
            arrived, terms = lax.optimization_barrier((arrived, terms))
        partial = sum_arrived(arrived)
        pieces.append(lax.psum_scatter(partial, "wz", scatter_dimension=0, tiled=True))
        if part < PARTS:
            arrived = send_along_x(terms, x_size)
    summed = jnp.concatenate(pieces, 0)
    mean_grad = summed / workers
    new_first = first_keep * first[0] + first_take * mean_grad
    new_second = second_keep * second[0] + second_take * mean_grad * mean_grad
    step_dir = new_first / first_fix / (jnp.sqrt(new_second / second_fix) + adam_eps)
    weight_step = rotate(step_dir) * sign_vec[None, :]
    new_weights = weights[0] - learn_rate * weight_step
    owners = lax.axis_size("tensor")
    piece_width = new_weights.shape[1] // owners
    narrow = new_weights.astype(jnp.bfloat16).reshape(blocks, owners, piece_width)
    slab_view = jnp.transpose(narrow, (1, 0, 2))
    slot_lists = slots[0, 0]
    used_counts = counts[0, 0]
    chosen_pieces = select_pieces(slab_view, slot_lists, used_counts)
    arrived = lax.all_to_all(chosen_pieces, "tensor", split_axis=0, concat_axis=0, tiled=True)
    return (new_first[None], new_second[None], new_weights[None], arrived[None, None])


def solution(mesh):
    dp_size, tensor_size = mesh.devices.shape
    split_mesh = Mesh(
        mesh.devices.reshape(X_CHIPS, dp_size // X_CHIPS, tensor_size), WORKERS + ("tensor",)
    )
    return jax.shard_map(
        per_device,
        mesh=split_mesh,
        in_specs=(
            P(WORKERS, "tensor", None, None),
            P("tensor", None),
            P(WORKERS, "tensor", None),
            P("tensor", WORKERS, None),
            P("tensor", WORKERS, None),
            P("tensor", WORKERS, None),
            P(WORKERS, "tensor", None, None),
            P(WORKERS, "tensor", None),
        ),
        out_specs=(
            P("tensor", WORKERS, None),
            P("tensor", WORKERS, None),
            P("tensor", WORKERS, None),
            P(WORKERS, "tensor", None, None, None),
        ),
        check_vma=False,
    )
```

```python
import math

import jax
import jax.numpy as jnp
from jax import lax
from jax.experimental import pallas as pl
from jax.experimental.pallas import tpu as pltpu
from jax.sharding import Mesh
from jax.sharding import PartitionSpec as P

HA = 32
HB = 128
ROW_TILE = 256
X_CHIPS = 4
Z_FIRST_ROWS = 8
WORKERS = ("wx", "wz")


first_keep = 0.9
first_take = 0.1
second_keep = 0.95
second_take = 0.05
first_fix = 1.0 - 0.9**10
second_fix = 1.0 - 0.95**10
adam_eps = 1e-08
learn_rate = 0.2


def walsh_table(table_order):
    positions = jnp.arange(table_order, dtype=jnp.int32)
    common_bits = jnp.bitwise_and(positions[:, None], positions[None, :])
    parity_sum = jnp.zeros((table_order, table_order), jnp.int32)
    for bit_level in range(max(table_order.bit_length() - 1, 1)):
        parity_sum = parity_sum + jnp.bitwise_and(jnp.right_shift(common_bits, bit_level), 1)
    return (1 - 2 * jnp.bitwise_and(parity_sum, 1)).astype(jnp.float32)


def rotate(flat_rows):
    count_rows = flat_rows.shape[0]
    cube_rows = flat_rows.reshape(count_rows, HA, HB)
    cube_rows = jnp.einsum(
        "rab,bc->rac", cube_rows, walsh_table(HB), precision=lax.Precision.HIGHEST
    )
    cube_rows = jnp.einsum(
        "ka,rac->rkc", walsh_table(HA), cube_rows, precision=lax.Precision.HIGHEST
    )
    return cube_rows.reshape(count_rows, HA * HB) / math.sqrt(HA * HB)


def half_power(shift_vals):
    unit_scale = jnp.ones(shift_vals.shape, jnp.float32)
    factor = 0.5
    for bit_level in range(5):
        chosen = jnp.bitwise_and(jnp.right_shift(shift_vals, bit_level), 1) == 1
        unit_scale = unit_scale * jnp.where(chosen, factor, 1.0).astype(jnp.float32)
        factor = factor * factor
    return unit_scale


def butterfly(blocks):
    blocks = list(blocks)
    span = 1
    while span < len(blocks):
        for start in range(0, len(blocks), 2 * span):
            for j in range(start, start + span):
                u, v = blocks[j], blocks[j + span]
                blocks[j], blocks[j + span] = u + v, u - v
        span *= 2
    return blocks


def code_kernel(x_ref, w_ref, up_ref, dn_ref, o_ref, y_ref):
    for a in range(HA):
        cols = slice(a * HB, (a + 1) * HB)
        y_ref[:, cols] = jnp.dot(x_ref[:, cols], w_ref[a], preferred_element_type=jnp.float32)

    def row_group(g, carry):
        rows = pl.ds(pl.multiple_of(g * 8, 8), 8)
        blocks = butterfly([y_ref[rows, a * HB:(a + 1) * HB] for a in range(HA)])
        up = up_ref[rows, :]
        dn = dn_ref[rows, :]
        for a in range(HA):
            coded = jnp.clip(blocks[a] * up, -127.0, 127.0).astype(jnp.bfloat16)
            o_ref[rows, a * HB:(a + 1) * HB] = (coded.astype(jnp.float32) * dn).astype(o_ref.dtype)
        return carry

    lax.fori_loop(0, x_ref.shape[0] // 8, row_group, 0)


def decoded_terms(grad_rows, signed_walsh, up_scale, down_scale):
    rows, width = grad_rows.shape
    return pl.pallas_call(
        code_kernel,
        grid=(rows // ROW_TILE,),
        in_specs=[
            pl.BlockSpec((ROW_TILE, width), lambda i: (i, 0)),
            pl.BlockSpec((HA, HB, HB), lambda i: (0, 0, 0)),
            pl.BlockSpec((ROW_TILE, 1), lambda i: (i, 0)),
            pl.BlockSpec((ROW_TILE, 1), lambda i: (i, 0)),
        ],
        out_specs=pl.BlockSpec((ROW_TILE, width), lambda i: (i, 0)),
        out_shape=jax.ShapeDtypeStruct((rows, width), jnp.bfloat16),
        scratch_shapes=[pltpu.VMEM((ROW_TILE, width), jnp.float32)],
        cost_estimate=pl.CostEstimate(
            flops=2 * rows * width * HB + 8 * rows * width,
            transcendentals=0,
            bytes_accessed=rows * width * 4,
        ),
    )(grad_rows, signed_walsh, up_scale, down_scale)


def send_along(axis, pieces, size, dim):
    mine = lax.axis_index(axis)
    arrived = [lax.dynamic_index_in_dim(pieces, mine, dim, keepdims=False)]
    for step in range(1, size):
        outgoing = lax.dynamic_index_in_dim(pieces, (mine + step) % size, dim, keepdims=False)
        pairs = [(i, (i + step) % size) for i in range(size)]
        arrived.append(lax.ppermute(outgoing, axis, pairs))
    return arrived


def sum_arrived(arrived):
    partial = arrived[0].astype(jnp.float32)
    for piece in arrived[1:]:
        partial = partial + piece.astype(jnp.float32)
    return partial


def select_pieces(slab_view, slot_lists, used_counts):
    gathered = jnp.take_along_axis(slab_view, slot_lists[:, :, None], axis=1)
    live_slots = lax.broadcasted_iota(jnp.int32, slot_lists.shape, 1) < used_counts[:, None]
    return jnp.where(live_slots[:, :, None], gathered, jnp.zeros((), jnp.bfloat16))


def per_device(grads, signs, shifts, first, second, weights, slots, counts):
    sign_vec = (2 * signs[0] - 1).astype(jnp.float32)
    grad_rows = grads[0, 0]
    shift_rows = shifts[0, 0]
    blocks = first.shape[1]
    signed_walsh = (sign_vec.reshape(HA, HB, 1) * walsh_table(HB)[None]).astype(jnp.bfloat16)
    unit_scale = half_power(shift_rows)[:, None]
    up_scale = (1.0 / unit_scale) / math.sqrt(HA * HB)
    terms = decoded_terms(grad_rows, signed_walsh, up_scale, unit_scale)
    x_size = lax.axis_size("wx")
    z_size = lax.axis_size("wz")
    workers = x_size * z_size
    by_dest = terms.reshape(x_size, z_size, blocks, -1)
    x_rows = blocks - Z_FIRST_ROWS
    x_arrived = send_along("wx", by_dest[:, :, :x_rows], x_size, 0)
    z_arrived = send_along("wz", by_dest[:, :, x_rows:], z_size, 1)
    x_arrived, z_arrived = lax.optimization_barrier((x_arrived, z_arrived))
    x_first = sum_arrived(x_arrived)
    x_first = lax.psum_scatter(x_first.reshape(z_size * x_rows, -1), "wz", scatter_dimension=0, tiled=True)
    z_first = sum_arrived(send_along("wx", sum_arrived(z_arrived), x_size, 0))
    summed = jnp.concatenate([x_first, z_first], 0)
    mean_grad = summed / workers
    new_first = first_keep * first[0] + first_take * mean_grad
    new_second = second_keep * second[0] + second_take * mean_grad * mean_grad
    step_dir = new_first / first_fix / (jnp.sqrt(new_second / second_fix) + adam_eps)
    weight_step = rotate(step_dir) * sign_vec[None, :]
    new_weights = weights[0] - learn_rate * weight_step
    owners = lax.axis_size("tensor")
    piece_width = new_weights.shape[1] // owners
    narrow = new_weights.astype(jnp.bfloat16).reshape(blocks, owners, piece_width)
    slab_view = jnp.transpose(narrow, (1, 0, 2))
    slot_lists = slots[0, 0]
    used_counts = counts[0, 0]
    chosen_pieces = select_pieces(slab_view, slot_lists, used_counts)
    arrived = lax.all_to_all(chosen_pieces, "tensor", split_axis=0, concat_axis=0, tiled=True)
    return (new_first[None], new_second[None], new_weights[None], arrived[None, None])


def solution(mesh):
    dp_size, tensor_size = mesh.devices.shape
    split_mesh = Mesh(
        mesh.devices.reshape(X_CHIPS, dp_size // X_CHIPS, tensor_size), WORKERS + ("tensor",)
    )
    return jax.shard_map(
        per_device,
        mesh=split_mesh,
        in_specs=(
            P(WORKERS, "tensor", None, None),
            P("tensor", None),
            P(WORKERS, "tensor", None),
            P("tensor", WORKERS, None),
            P("tensor", WORKERS, None),
            P("tensor", WORKERS, None),
            P(WORKERS, "tensor", None, None),
            P(WORKERS, "tensor", None),
        ),
        out_specs=(
            P("tensor", WORKERS, None),
            P("tensor", WORKERS, None),
            P("tensor", WORKERS, None),
            P(WORKERS, "tensor", None, None, None),
        ),
        check_vma=False,
    )
```

```python
import functools
import math

import jax
import jax.numpy as jnp
from jax import lax
from jax.experimental import pallas as pl
from jax.experimental.pallas import tpu as pltpu
from jax.sharding import Mesh
from jax.sharding import PartitionSpec as P

HA = 32
HB = 128
ROW_TILE = 256
X_CHIPS = 4
PARTS = 2
WORKERS = ("wx", "wz")


first_keep = 0.9
first_take = 0.1
second_keep = 0.95
second_take = 0.05
first_fix = 1.0 - 0.9**10
second_fix = 1.0 - 0.95**10
adam_eps = 1e-08
learn_rate = 0.2


def walsh_table(table_order):
    positions = jnp.arange(table_order, dtype=jnp.int32)
    common_bits = jnp.bitwise_and(positions[:, None], positions[None, :])
    parity_sum = jnp.zeros((table_order, table_order), jnp.int32)
    for bit_level in range(max(table_order.bit_length() - 1, 1)):
        parity_sum = parity_sum + jnp.bitwise_and(jnp.right_shift(common_bits, bit_level), 1)
    return (1 - 2 * jnp.bitwise_and(parity_sum, 1)).astype(jnp.float32)


def rotate(flat_rows):
    count_rows = flat_rows.shape[0]
    cube_rows = flat_rows.reshape(count_rows, HA, HB)
    cube_rows = jnp.einsum(
        "rab,bc->rac", cube_rows, walsh_table(HB), precision=lax.Precision.HIGHEST
    )
    cube_rows = jnp.einsum(
        "ka,rac->rkc", walsh_table(HA), cube_rows, precision=lax.Precision.HIGHEST
    )
    return cube_rows.reshape(count_rows, HA * HB) / math.sqrt(HA * HB)


def half_power(shift_vals):
    unit_scale = jnp.ones(shift_vals.shape, jnp.float32)
    factor = 0.5
    for bit_level in range(5):
        chosen = jnp.bitwise_and(jnp.right_shift(shift_vals, bit_level), 1) == 1
        unit_scale = unit_scale * jnp.where(chosen, factor, 1.0).astype(jnp.float32)
        factor = factor * factor
    return unit_scale


def butterfly(blocks):
    blocks = list(blocks)
    span = 1
    while span < len(blocks):
        for start in range(0, len(blocks), 2 * span):
            for j in range(start, start + span):
                u, v = blocks[j], blocks[j + span]
                blocks[j], blocks[j + span] = u + v, u - v
        span *= 2
    return blocks


def exact_powers(shift_vals):
    up = jnp.ones(shift_vals.shape, jnp.float32)
    down = jnp.ones(shift_vals.shape, jnp.float32)
    factor = 2.0
    for bit_level in range(5):
        chosen = jnp.bitwise_and(jnp.right_shift(shift_vals, bit_level), 1) == 1
        up = up * jnp.where(chosen, factor, 1.0)
        down = down * jnp.where(chosen, 1.0 / factor, 1.0)
        factor = factor * factor
    return up, down


def code_rows(y_ref, sh_ref, o_ref, group_rows, g, carry):
    rows = pl.ds(pl.multiple_of(g * 8, 8), 8)
    dest = g // (group_rows // 8)
    within = pl.ds(pl.multiple_of((g % (group_rows // 8)) * 8, 8), 8)
    blocks = butterfly([y_ref[rows, a * HB:(a + 1) * HB] for a in range(HA)])
    up, dn = exact_powers(sh_ref[dest, within, :])
    up = up * (1.0 / math.sqrt(HA * HB))
    for a in range(HA):
        coded = jnp.clip(blocks[a] * up, -127.0, 127.0).astype(jnp.bfloat16)
        o_ref[rows, a * HB:(a + 1) * HB] = (coded.astype(jnp.float32) * dn).astype(o_ref.dtype)
    return carry


def code_kernel(mx_ref, x_ref, sg_ref, w_ref, sh_ref, *refs):
    out_refs, y_ref = refs[:-1], refs[-1]
    step = pl.program_id(0)
    groups, group_rows, _ = x_ref.shape
    for a in range(HA):
        cols = slice(a * HB, (a + 1) * HB)
        lhs = (x_ref[:, :, cols] * sg_ref[:, cols]).reshape(groups * group_rows, HB)
        y_ref[:, cols] = jnp.dot(lhs, w_ref[...], preferred_element_type=jnp.float32)
    for k, o_ref in enumerate(out_refs):

        @pl.when(step == k)
        def _(o_ref=o_ref):
            coder = functools.partial(code_rows, y_ref, sh_ref, o_ref, group_rows)
            lax.fori_loop(0, groups * group_rows // 8, coder, 0)


def decoded_terms(grad_groups, sign_row, walsh, shift_groups, part, x_size):
    dests, _, part_rows, width = grad_groups.shape
    per_x = dests // x_size
    my_x = jnp.reshape(lax.axis_index("wx"), (1,)).astype(jnp.int32)
    tile = lambda i, mx: ((mx[0] + i) % x_size, part, 0, 0)
    whole = lambda i, mx: (0, 0)
    out_rows = per_x * part_rows
    return pl.pallas_call(
        code_kernel,
        grid_spec=pltpu.PrefetchScalarGridSpec(
            num_scalar_prefetch=1,
            grid=(x_size,),
            in_specs=[
                pl.BlockSpec((per_x, None, part_rows, width), tile),
                pl.BlockSpec((1, width), whole),
                pl.BlockSpec((HB, HB), whole),
                pl.BlockSpec((per_x, None, part_rows, 1), tile),
            ],
            out_specs=[pl.BlockSpec((out_rows, width), whole) for _ in range(x_size)],
            scratch_shapes=[pltpu.VMEM((out_rows, width), jnp.float32)],
        ),
        out_shape=[jax.ShapeDtypeStruct((out_rows, width), jnp.bfloat16) for _ in range(x_size)],
        cost_estimate=pl.CostEstimate(
            flops=2 * dests * part_rows * width * HB + 8 * dests * part_rows * width,
            transcendentals=0,
            bytes_accessed=dests * part_rows * width * 4,
        ),
    )(my_x, grad_groups, sign_row, walsh, shift_groups)


def send_along_x(terms, x_size):
    arrived = [terms[0]]
    for step in range(1, x_size):
        pairs = [(i, (i + step) % x_size) for i in range(x_size)]
        arrived.append(lax.ppermute(terms[step], "wx", pairs))
    return arrived


def sum_arrived(arrived):
    partial = arrived[0].astype(jnp.float32)
    for piece in arrived[1:]:
        partial = partial + piece.astype(jnp.float32)
    return partial


def select_pieces(slab_view, slot_lists, used_counts):
    gathered = jnp.take_along_axis(slab_view, slot_lists[:, :, None], axis=1)
    live_slots = lax.broadcasted_iota(jnp.int32, slot_lists.shape, 1) < used_counts[:, None]
    return jnp.where(live_slots[:, :, None], gathered, jnp.zeros((), jnp.bfloat16))


def per_device(grads, signs, shifts, first, second, weights, slots, counts):
    sign_vec = (2 * signs[0] - 1).astype(jnp.float32)
    grad_rows = grads[0, 0]
    shift_rows = shifts[0, 0]
    blocks = first.shape[1]
    sign_row = sign_vec.astype(jnp.bfloat16)[None, :]
    walsh = walsh_table(HB).astype(jnp.bfloat16)
    x_size = lax.axis_size("wx")
    dests = x_size * lax.axis_size("wz")
    workers = dests
    part_rows = blocks // PARTS
    as_groups = lambda rows: rows.reshape(dests, PARTS, part_rows, rows.shape[-1])
    grad_groups = as_groups(grad_rows)
    shift_groups = as_groups(shift_rows[:, None])
    pieces = []
    terms = decoded_terms(grad_groups, sign_row, walsh, shift_groups, 0, x_size)
    arrived = send_along_x(terms, x_size)
    for part in range(1, PARTS + 1):
        if part < PARTS:
            terms = decoded_terms(grad_groups, sign_row, walsh, shift_groups, part, x_size)
            arrived, terms = lax.optimization_barrier((arrived, terms))
        partial = sum_arrived(arrived)
        pieces.append(lax.psum_scatter(partial, "wz", scatter_dimension=0, tiled=True))
        if part < PARTS:
            arrived = send_along_x(terms, x_size)
    summed = jnp.concatenate(pieces, 0)
    mean_grad = summed / workers
    new_first = first_keep * first[0] + first_take * mean_grad
    new_second = second_keep * second[0] + second_take * mean_grad * mean_grad
    step_dir = new_first / first_fix / (jnp.sqrt(new_second / second_fix) + adam_eps)
    weight_step = rotate(step_dir) * sign_vec[None, :]
    new_weights = weights[0] - learn_rate * weight_step
    owners = lax.axis_size("tensor")
    piece_width = new_weights.shape[1] // owners
    narrow = new_weights.astype(jnp.bfloat16).reshape(blocks, owners, piece_width)
    slab_view = jnp.transpose(narrow, (1, 0, 2))
    slot_lists = slots[0, 0]
    used_counts = counts[0, 0]
    chosen_pieces = select_pieces(slab_view, slot_lists, used_counts)
    arrived = lax.all_to_all(chosen_pieces, "tensor", split_axis=0, concat_axis=0, tiled=True)
    return (new_first[None], new_second[None], new_weights[None], arrived[None, None])


def solution(mesh):
    dp_size, tensor_size = mesh.devices.shape
    split_mesh = Mesh(
        mesh.devices.reshape(X_CHIPS, dp_size // X_CHIPS, tensor_size), WORKERS + ("tensor",)
    )
    return jax.shard_map(
        per_device,
        mesh=split_mesh,
        in_specs=(
            P(WORKERS, "tensor", None, None),
            P("tensor", None),
            P(WORKERS, "tensor", None),
            P("tensor", WORKERS, None),
            P("tensor", WORKERS, None),
            P("tensor", WORKERS, None),
            P(WORKERS, "tensor", None, None),
            P(WORKERS, "tensor", None),
        ),
        out_specs=(
            P("tensor", WORKERS, None),
            P("tensor", WORKERS, None),
            P("tensor", WORKERS, None),
            P(WORKERS, "tensor", None, None, None),
        ),
        check_vma=False,
    )
```

```python
import functools
import math

import jax
import numpy as np
import jax.numpy as jnp
from jax import lax
from jax.experimental import pallas as pl
from jax.experimental.pallas import tpu as pltpu
from jax.sharding import Mesh
from jax.sharding import PartitionSpec as P

HA = 32
HB = 128
ROW_TILE = 256
X_CHIPS = 4
PARTS = 2
WORKERS = ("wx", "wz")


first_keep = 0.9
first_take = 0.1
second_keep = 0.95
second_take = 0.05
first_fix = 1.0 - 0.9**10
second_fix = 1.0 - 0.95**10
adam_eps = 1e-08
learn_rate = 0.2


def walsh_table(table_order):
    positions = jnp.arange(table_order, dtype=jnp.int32)
    common_bits = jnp.bitwise_and(positions[:, None], positions[None, :])
    parity_sum = jnp.zeros((table_order, table_order), jnp.int32)
    for bit_level in range(max(table_order.bit_length() - 1, 1)):
        parity_sum = parity_sum + jnp.bitwise_and(jnp.right_shift(common_bits, bit_level), 1)
    return (1 - 2 * jnp.bitwise_and(parity_sum, 1)).astype(jnp.float32)


def rotate(flat_rows):
    count_rows = flat_rows.shape[0]
    cube_rows = flat_rows.reshape(count_rows, HA, HB)
    cube_rows = jnp.einsum(
        "rab,bc->rac", cube_rows, walsh_table(HB), precision=lax.Precision.HIGHEST
    )
    cube_rows = jnp.einsum(
        "ka,rac->rkc", walsh_table(HA), cube_rows, precision=lax.Precision.HIGHEST
    )
    return cube_rows.reshape(count_rows, HA * HB) / math.sqrt(HA * HB)


def half_power(shift_vals):
    unit_scale = jnp.ones(shift_vals.shape, jnp.float32)
    factor = 0.5
    for bit_level in range(5):
        chosen = jnp.bitwise_and(jnp.right_shift(shift_vals, bit_level), 1) == 1
        unit_scale = unit_scale * jnp.where(chosen, factor, 1.0).astype(jnp.float32)
        factor = factor * factor
    return unit_scale


def butterfly(blocks):
    blocks = list(blocks)
    span = 1
    while span < len(blocks):
        for start in range(0, len(blocks), 2 * span):
            for j in range(start, start + span):
                u, v = blocks[j], blocks[j + span]
                blocks[j], blocks[j + span] = u + v, u - v
        span *= 2
    return blocks


def exact_powers(shift_vals):
    up = jnp.ones(shift_vals.shape, jnp.float32)
    down = jnp.ones(shift_vals.shape, jnp.float32)
    factor = 2.0
    for bit_level in range(5):
        chosen = jnp.bitwise_and(jnp.right_shift(shift_vals, bit_level), 1) == 1
        up = up * jnp.where(chosen, factor, 1.0)
        down = down * jnp.where(chosen, 1.0 / factor, 1.0)
        factor = factor * factor
    return up, down


def walsh_constant(table_order):
    positions = np.arange(table_order)
    common_bits = np.bitwise_and(positions[:, None], positions[None, :])
    parity = np.zeros((table_order, table_order), np.int64)
    for bit_level in range(max(table_order.bit_length() - 1, 1)):
        parity = parity + np.right_shift(common_bits, bit_level) % 2
    return jnp.asarray((1 - 2 * (parity % 2)).astype(np.float32), dtype=jnp.bfloat16)


def code_rows(y_ref, sh_ref, o_ref, group_rows, first_row, g, carry):
    rows = pl.ds(pl.multiple_of(g * 8, 8), 8)
    dest = g // (group_rows // 8)
    within = (g % (group_rows // 8)) * 8
    blocks = butterfly([y_ref[rows, a * HB:(a + 1) * HB] for a in range(HA)])
    base = first_row(dest) + within
    row_ids = lax.broadcasted_iota(jnp.int32, (8, 1), 0)
    shift_col = jnp.zeros((8, 1), jnp.int32)
    for j in range(8):
        shift_col = jnp.where(row_ids == j, sh_ref[0, 0, base + j], shift_col)
    up, dn = exact_powers(shift_col)
    up = up * (1.0 / math.sqrt(HA * HB))
    for a in range(HA):
        coded = jnp.clip(blocks[a] * up, -127.0, 127.0).astype(jnp.bfloat16)
        o_ref[rows, a * HB:(a + 1) * HB] = (coded.astype(jnp.float32) * dn).astype(o_ref.dtype)
    return carry


def code_kernel(part, x_size, mx_ref, sh_ref, x_ref, sg_ref, w_ref, *refs):
    out_refs, y_ref = refs[:-1], refs[-1]
    step = pl.program_id(0)
    groups, group_rows, _ = x_ref.shape
    dest_rows = group_rows * PARTS
    first_dest = ((mx_ref[0] + step) % x_size) * groups
    first_row = lambda dest: (first_dest + dest) * dest_rows + part * group_rows
    for a in range(HA):
        cols = slice(a * HB, (a + 1) * HB)
        sign = (2 * sg_ref[:, cols] - 1).astype(jnp.float32).astype(jnp.bfloat16)
        lhs = (x_ref[:, :, cols] * sign).reshape(groups * group_rows, HB)
        y_ref[:, cols] = jnp.dot(lhs, w_ref[...], preferred_element_type=jnp.float32)
    for k, o_ref in enumerate(out_refs):

        @pl.when(step == k)
        def _(o_ref=o_ref):
            coder = functools.partial(code_rows, y_ref, sh_ref, o_ref, group_rows, first_row)
            lax.fori_loop(0, groups * group_rows // 8, coder, 0)


def decoded_terms(grad_groups, signs, walsh, shifts, part, x_size):
    dests, _, part_rows, width = grad_groups.shape
    per_x = dests // x_size
    my_x = jnp.reshape(lax.axis_index("wx"), (1,)).astype(jnp.int32)
    tile = lambda i, mx, sh: ((mx[0] + i) % x_size, part, 0, 0)
    whole = lambda i, mx, sh: (0, 0)
    out_rows = per_x * part_rows
    return pl.pallas_call(
        functools.partial(code_kernel, part, x_size),
        grid_spec=pltpu.PrefetchScalarGridSpec(
            num_scalar_prefetch=2,
            grid=(x_size,),
            in_specs=[
                pl.BlockSpec((per_x, None, part_rows, width), tile),
                pl.BlockSpec((1, width), whole),
                pl.BlockSpec((HB, HB), whole),
            ],
            out_specs=[pl.BlockSpec((out_rows, width), whole) for _ in range(x_size)],
            scratch_shapes=[pltpu.VMEM((out_rows, width), jnp.float32)],
        ),
        out_shape=[jax.ShapeDtypeStruct((out_rows, width), jnp.bfloat16) for _ in range(x_size)],
        cost_estimate=pl.CostEstimate(
            flops=2 * dests * part_rows * width * HB + 8 * dests * part_rows * width,
            transcendentals=0,
            bytes_accessed=dests * part_rows * width * 4,
        ),
    )(my_x, shifts, grad_groups, signs, walsh)


def send_along_x(terms, x_size):
    arrived = [terms[0]]
    for step in range(1, x_size):
        pairs = [(i, (i + step) % x_size) for i in range(x_size)]
        arrived.append(lax.ppermute(terms[step], "wx", pairs))
    return arrived


def sum_arrived(arrived):
    partial = arrived[0].astype(jnp.float32)
    for piece in arrived[1:]:
        partial = partial + piece.astype(jnp.float32)
    return partial


def select_pieces(slab_view, slot_lists, used_counts):
    gathered = jnp.take_along_axis(slab_view, slot_lists[:, :, None], axis=1)
    live_slots = lax.broadcasted_iota(jnp.int32, slot_lists.shape, 1) < used_counts[:, None]
    return jnp.where(live_slots[:, :, None], gathered, jnp.zeros((), jnp.bfloat16))


def per_device(grads, signs, shifts, first, second, weights, slots, counts):
    sign_vec = (2 * signs[0] - 1).astype(jnp.float32)
    grad_rows = grads[0, 0]
    blocks = first.shape[1]
    walsh = walsh_constant(HB)
    x_size = lax.axis_size("wx")
    dests = x_size * lax.axis_size("wz")
    workers = dests
    part_rows = blocks // PARTS
    grad_groups = grad_rows.reshape(dests, PARTS, part_rows, grad_rows.shape[-1])
    pieces = []
    terms = decoded_terms(grad_groups, signs, walsh, shifts, 0, x_size)
    arrived = send_along_x(terms, x_size)
    for part in range(1, PARTS + 1):
        if part < PARTS:
            terms = decoded_terms(grad_groups, signs, walsh, shifts, part, x_size)
            arrived, terms = lax.optimization_barrier((arrived, terms))
        partial = sum_arrived(arrived)
        pieces.append(lax.psum_scatter(partial, "wz", scatter_dimension=0, tiled=True))
        if part < PARTS:
            arrived = send_along_x(terms, x_size)
    summed = jnp.concatenate(pieces, 0)
    mean_grad = summed / workers
    new_first = first_keep * first[0] + first_take * mean_grad
    new_second = second_keep * second[0] + second_take * mean_grad * mean_grad
    step_dir = new_first / first_fix / (jnp.sqrt(new_second / second_fix) + adam_eps)
    weight_step = rotate(step_dir) * sign_vec[None, :]
    new_weights = weights[0] - learn_rate * weight_step
    owners = lax.axis_size("tensor")
    piece_width = new_weights.shape[1] // owners
    narrow = new_weights.astype(jnp.bfloat16).reshape(blocks, owners, piece_width)
    slab_view = jnp.transpose(narrow, (1, 0, 2))
    slot_lists = slots[0, 0]
    used_counts = counts[0, 0]
    chosen_pieces = select_pieces(slab_view, slot_lists, used_counts)
    arrived = lax.all_to_all(chosen_pieces, "tensor", split_axis=0, concat_axis=0, tiled=True)
    return (new_first[None], new_second[None], new_weights[None], arrived[None, None])


def solution(mesh):
    dp_size, tensor_size = mesh.devices.shape
    split_mesh = Mesh(
        mesh.devices.reshape(X_CHIPS, dp_size // X_CHIPS, tensor_size), WORKERS + ("tensor",)
    )
    return jax.shard_map(
        per_device,
        mesh=split_mesh,
        in_specs=(
            P(WORKERS, "tensor", None, None),
            P("tensor", None),
            P(WORKERS, "tensor", None),
            P("tensor", WORKERS, None),
            P("tensor", WORKERS, None),
            P("tensor", WORKERS, None),
            P(WORKERS, "tensor", None, None),
            P(WORKERS, "tensor", None),
        ),
        out_specs=(
            P("tensor", WORKERS, None),
            P("tensor", WORKERS, None),
            P("tensor", WORKERS, None),
            P(WORKERS, "tensor", None, None, None),
        ),
        check_vma=False,
    )
```

```python
import functools
import math

import jax
import numpy as np
import jax.numpy as jnp
from jax import lax
from jax.experimental import pallas as pl
from jax.experimental.pallas import tpu as pltpu
from jax.sharding import Mesh
from jax.sharding import PartitionSpec as P

HA = 32
HB = 128
ROW_TILE = 256
X_CHIPS = 4
PARTS = 2
WORKERS = ("wx", "wz")


first_keep = 0.9
first_take = 0.1
second_keep = 0.95
second_take = 0.05
first_fix = 1.0 - 0.9**10
second_fix = 1.0 - 0.95**10
adam_eps = 1e-08
learn_rate = 0.2


def walsh_table(table_order):
    positions = jnp.arange(table_order, dtype=jnp.int32)
    common_bits = jnp.bitwise_and(positions[:, None], positions[None, :])
    parity_sum = jnp.zeros((table_order, table_order), jnp.int32)
    for bit_level in range(max(table_order.bit_length() - 1, 1)):
        parity_sum = parity_sum + jnp.bitwise_and(jnp.right_shift(common_bits, bit_level), 1)
    return (1 - 2 * jnp.bitwise_and(parity_sum, 1)).astype(jnp.float32)


def rotate(flat_rows):
    count_rows = flat_rows.shape[0]
    cube_rows = flat_rows.reshape(count_rows, HA, HB)
    cube_rows = jnp.einsum(
        "rab,bc->rac", cube_rows, walsh_table(HB), precision=lax.Precision.HIGHEST
    )
    cube_rows = jnp.einsum(
        "ka,rac->rkc", walsh_table(HA), cube_rows, precision=lax.Precision.HIGHEST
    )
    return cube_rows.reshape(count_rows, HA * HB) / math.sqrt(HA * HB)


def half_power(shift_vals):
    unit_scale = jnp.ones(shift_vals.shape, jnp.float32)
    factor = 0.5
    for bit_level in range(5):
        chosen = jnp.bitwise_and(jnp.right_shift(shift_vals, bit_level), 1) == 1
        unit_scale = unit_scale * jnp.where(chosen, factor, 1.0).astype(jnp.float32)
        factor = factor * factor
    return unit_scale


def butterfly(blocks):
    blocks = list(blocks)
    span = 1
    while span < len(blocks):
        for start in range(0, len(blocks), 2 * span):
            for j in range(start, start + span):
                u, v = blocks[j], blocks[j + span]
                blocks[j], blocks[j + span] = u + v, u - v
        span *= 2
    return blocks


def exact_powers(shift_vals):
    up = jnp.ones(shift_vals.shape, jnp.float32)
    down = jnp.ones(shift_vals.shape, jnp.float32)
    factor = 2.0
    for bit_level in range(5):
        chosen = jnp.bitwise_and(jnp.right_shift(shift_vals, bit_level), 1) == 1
        up = up * jnp.where(chosen, factor, 1.0)
        down = down * jnp.where(chosen, 1.0 / factor, 1.0)
        factor = factor * factor
    return up, down


def walsh_constant(table_order):
    positions = np.arange(table_order)
    common_bits = np.bitwise_and(positions[:, None], positions[None, :])
    parity = np.zeros((table_order, table_order), np.int64)
    for bit_level in range(max(table_order.bit_length() - 1, 1)):
        parity = parity + np.right_shift(common_bits, bit_level) % 2
    return jnp.asarray((1 - 2 * (parity % 2)).astype(np.float32), dtype=jnp.bfloat16)


def code_rows(y_ref, sh_ref, o_ref, group_rows, first_row, g, carry):
    rows = pl.ds(pl.multiple_of(g * 8, 8), 8)
    dest = g // (group_rows // 8)
    within = (g % (group_rows // 8)) * 8
    blocks = butterfly([y_ref[rows, a * HB:(a + 1) * HB] for a in range(HA)])
    base = first_row(dest) + within
    row_ids = lax.broadcasted_iota(jnp.int32, (8, 1), 0)
    shift_col = jnp.zeros((8, 1), jnp.int32)
    for j in range(8):
        shift_col = jnp.where(row_ids == j, sh_ref[0, 0, base + j], shift_col)
    up, dn = exact_powers(shift_col)
    up = up * (1.0 / math.sqrt(HA * HB))
    dn = dn.astype(jnp.bfloat16)
    for a in range(HA):
        coded = jnp.clip(blocks[a] * up, -127.0, 127.0).astype(jnp.bfloat16)
        o_ref[rows, a * HB:(a + 1) * HB] = (coded * dn).astype(o_ref.dtype)
    return carry


def code_kernel(part, x_size, mx_ref, sh_ref, x_ref, sg_ref, w_ref, *refs):
    out_refs, y_ref = refs[:-1], refs[-1]
    step = pl.program_id(0)
    groups, group_rows, _ = x_ref.shape
    dest_rows = group_rows * PARTS
    first_dest = ((mx_ref[0] + step) % x_size) * groups
    first_row = lambda dest: (first_dest + dest) * dest_rows + part * group_rows
    for a in range(HA):
        cols = slice(a * HB, (a + 1) * HB)
        sign = (2 * sg_ref[:, cols] - 1).astype(jnp.float32).astype(jnp.bfloat16)
        lhs = (x_ref[:, :, cols] * sign).reshape(groups * group_rows, HB)
        y_ref[:, cols] = jnp.dot(lhs, w_ref[...], preferred_element_type=jnp.float32)
    for k, o_ref in enumerate(out_refs):

        @pl.when(step == k)
        def _(o_ref=o_ref):
            coder = functools.partial(code_rows, y_ref, sh_ref, o_ref, group_rows, first_row)
            lax.fori_loop(0, groups * group_rows // 8, coder, 0)


def decoded_terms(grad_groups, signs, walsh, shifts, part, x_size):
    dests, _, part_rows, width = grad_groups.shape
    per_x = dests // x_size
    my_x = jnp.reshape(lax.axis_index("wx"), (1,)).astype(jnp.int32)
    tile = lambda i, mx, sh: ((mx[0] + i) % x_size, part, 0, 0)
    whole = lambda i, mx, sh: (0, 0)
    out_rows = per_x * part_rows
    return pl.pallas_call(
        functools.partial(code_kernel, part, x_size),
        grid_spec=pltpu.PrefetchScalarGridSpec(
            num_scalar_prefetch=2,
            grid=(x_size,),
            in_specs=[
                pl.BlockSpec((per_x, None, part_rows, width), tile),
                pl.BlockSpec((1, width), whole),
                pl.BlockSpec((HB, HB), whole),
            ],
            out_specs=[pl.BlockSpec((out_rows, width), whole) for _ in range(x_size)],
            scratch_shapes=[pltpu.VMEM((out_rows, width), jnp.float32)],
        ),
        out_shape=[jax.ShapeDtypeStruct((out_rows, width), jnp.bfloat16) for _ in range(x_size)],
        cost_estimate=pl.CostEstimate(
            flops=2 * dests * part_rows * width * HB + 8 * dests * part_rows * width,
            transcendentals=0,
            bytes_accessed=dests * part_rows * width * 4,
        ),
    )(my_x, shifts, grad_groups, signs, walsh)


def send_along_x(terms, x_size):
    arrived = [terms[0]]
    for step in range(1, x_size):
        pairs = [(i, (i + step) % x_size) for i in range(x_size)]
        arrived.append(lax.ppermute(terms[step], "wx", pairs))
    return arrived


def sum_arrived(arrived):
    partial = arrived[0].astype(jnp.float32)
    for piece in arrived[1:]:
        partial = partial + piece.astype(jnp.float32)
    return partial


def select_pieces(slab_view, slot_lists, used_counts):
    gathered = jnp.take_along_axis(slab_view, slot_lists[:, :, None], axis=1)
    live_slots = lax.broadcasted_iota(jnp.int32, slot_lists.shape, 1) < used_counts[:, None]
    return jnp.where(live_slots[:, :, None], gathered, jnp.zeros((), jnp.bfloat16))


def per_device(grads, signs, shifts, first, second, weights, slots, counts):
    sign_vec = (2 * signs[0] - 1).astype(jnp.float32)
    grad_rows = grads[0, 0]
    blocks = first.shape[1]
    walsh = walsh_constant(HB)
    x_size = lax.axis_size("wx")
    dests = x_size * lax.axis_size("wz")
    workers = dests
    part_rows = blocks // PARTS
    grad_groups = grad_rows.reshape(dests, PARTS, part_rows, grad_rows.shape[-1])
    pieces = []
    terms = decoded_terms(grad_groups, signs, walsh, shifts, 0, x_size)
    arrived = send_along_x(terms, x_size)
    for part in range(1, PARTS + 1):
        if part < PARTS:
            terms = decoded_terms(grad_groups, signs, walsh, shifts, part, x_size)
            arrived, terms = lax.optimization_barrier((arrived, terms))
        partial = sum_arrived(arrived)
        pieces.append(lax.psum_scatter(partial, "wz", scatter_dimension=0, tiled=True))
        if part < PARTS:
            arrived = send_along_x(terms, x_size)
    summed = jnp.concatenate(pieces, 0)
    mean_grad = summed / workers
    new_first = first_keep * first[0] + first_take * mean_grad
    new_second = second_keep * second[0] + second_take * mean_grad * mean_grad
    step_dir = new_first / first_fix / (jnp.sqrt(new_second / second_fix) + adam_eps)
    weight_step = rotate(step_dir) * sign_vec[None, :]
    new_weights = weights[0] - learn_rate * weight_step
    owners = lax.axis_size("tensor")
    piece_width = new_weights.shape[1] // owners
    narrow = new_weights.astype(jnp.bfloat16).reshape(blocks, owners, piece_width)
    slab_view = jnp.transpose(narrow, (1, 0, 2))
    slot_lists = slots[0, 0]
    used_counts = counts[0, 0]
    chosen_pieces = select_pieces(slab_view, slot_lists, used_counts)
    arrived = lax.all_to_all(chosen_pieces, "tensor", split_axis=0, concat_axis=0, tiled=True)
    return (new_first[None], new_second[None], new_weights[None], arrived[None, None])


def solution(mesh):
    dp_size, tensor_size = mesh.devices.shape
    split_mesh = Mesh(
        mesh.devices.reshape(X_CHIPS, dp_size // X_CHIPS, tensor_size), WORKERS + ("tensor",)
    )
    return jax.shard_map(
        per_device,
        mesh=split_mesh,
        in_specs=(
            P(WORKERS, "tensor", None, None),
            P("tensor", None),
            P(WORKERS, "tensor", None),
            P("tensor", WORKERS, None),
            P("tensor", WORKERS, None),
            P("tensor", WORKERS, None),
            P(WORKERS, "tensor", None, None),
            P(WORKERS, "tensor", None),
        ),
        out_specs=(
            P("tensor", WORKERS, None),
            P("tensor", WORKERS, None),
            P("tensor", WORKERS, None),
            P(WORKERS, "tensor", None, None, None),
        ),
        check_vma=False,
    )
```

```python
import functools
import math

import jax
import numpy as np
import jax.numpy as jnp
from jax import lax
from jax.experimental import pallas as pl
from jax.experimental.pallas import tpu as pltpu
from jax.sharding import Mesh
from jax.sharding import PartitionSpec as P

HA = 32
HB = 128
ROW_TILE = 256
X_CHIPS = 4
PARTS = 2
WORKERS = ("wx", "wz")


first_keep = 0.9
first_take = 0.1
second_keep = 0.95
second_take = 0.05
first_fix = 1.0 - 0.9**10
second_fix = 1.0 - 0.95**10
adam_eps = 1e-08
learn_rate = 0.2


def walsh_table(table_order):
    positions = jnp.arange(table_order, dtype=jnp.int32)
    common_bits = jnp.bitwise_and(positions[:, None], positions[None, :])
    parity_sum = jnp.zeros((table_order, table_order), jnp.int32)
    for bit_level in range(max(table_order.bit_length() - 1, 1)):
        parity_sum = parity_sum + jnp.bitwise_and(jnp.right_shift(common_bits, bit_level), 1)
    return (1 - 2 * jnp.bitwise_and(parity_sum, 1)).astype(jnp.float32)


def rotate(flat_rows):
    count_rows = flat_rows.shape[0]
    cube_rows = flat_rows.reshape(count_rows, HA, HB)
    cube_rows = jnp.einsum(
        "rab,bc->rac", cube_rows, walsh_table(HB), precision=lax.Precision.HIGHEST
    )
    cube_rows = jnp.einsum(
        "ka,rac->rkc", walsh_table(HA), cube_rows, precision=lax.Precision.HIGHEST
    )
    return cube_rows.reshape(count_rows, HA * HB) / math.sqrt(HA * HB)


def half_power(shift_vals):
    unit_scale = jnp.ones(shift_vals.shape, jnp.float32)
    factor = 0.5
    for bit_level in range(5):
        chosen = jnp.bitwise_and(jnp.right_shift(shift_vals, bit_level), 1) == 1
        unit_scale = unit_scale * jnp.where(chosen, factor, 1.0).astype(jnp.float32)
        factor = factor * factor
    return unit_scale


def butterfly(blocks):
    blocks = list(blocks)
    span = 1
    while span < len(blocks):
        for start in range(0, len(blocks), 2 * span):
            for j in range(start, start + span):
                u, v = blocks[j], blocks[j + span]
                blocks[j], blocks[j + span] = u + v, u - v
        span *= 2
    return blocks


def exact_powers(shift_vals):
    up = jnp.ones(shift_vals.shape, jnp.float32)
    down = jnp.ones(shift_vals.shape, jnp.float32)
    factor = 2.0
    for bit_level in range(5):
        chosen = jnp.bitwise_and(jnp.right_shift(shift_vals, bit_level), 1) == 1
        up = up * jnp.where(chosen, factor, 1.0)
        down = down * jnp.where(chosen, 1.0 / factor, 1.0)
        factor = factor * factor
    return up, down


def walsh_constant(table_order):
    positions = np.arange(table_order)
    common_bits = np.bitwise_and(positions[:, None], positions[None, :])
    parity = np.zeros((table_order, table_order), np.int64)
    for bit_level in range(max(table_order.bit_length() - 1, 1)):
        parity = parity + np.right_shift(common_bits, bit_level) % 2
    return jnp.asarray((1 - 2 * (parity % 2)).astype(np.float32), dtype=jnp.bfloat16)


def code_rows(y_ref, sh_ref, o_ref, group_rows, first_row, g, carry):
    rows = pl.ds(pl.multiple_of(g * 8, 8), 8)
    dest = g // (group_rows // 8)
    within = (g % (group_rows // 8)) * 8
    blocks = butterfly([y_ref[rows, a * HB:(a + 1) * HB] for a in range(HA)])
    base = first_row(dest) + within
    row_ids = lax.broadcasted_iota(jnp.int32, (8, 1), 0)
    shift_col = jnp.zeros((8, 1), jnp.int32)
    for j in range(8):
        shift_col = jnp.where(row_ids == j, sh_ref[0, 0, base + j], shift_col)
    up, dn = exact_powers(shift_col)
    up = up * (1.0 / math.sqrt(HA * HB))
    dn = dn.astype(jnp.bfloat16)
    for a in range(HA):
        coded = jnp.clip(blocks[a] * up, -127.0, 127.0).astype(jnp.bfloat16)
        o_ref[rows, a * HB:(a + 1) * HB] = (coded * dn).astype(o_ref.dtype)
    return carry


def code_kernel(part, x_size, mx_ref, sh_ref, x_ref, sg_ref, w_ref, *refs):
    out_refs, y_ref = refs[:-1], refs[-1]
    step = pl.program_id(0)
    groups, group_rows, _ = x_ref.shape
    dest_rows = group_rows * PARTS
    first_dest = ((mx_ref[0] + step) % x_size) * groups
    first_row = lambda dest: (first_dest + dest) * dest_rows + part * group_rows
    for a in range(HA):
        cols = slice(a * HB, (a + 1) * HB)
        sign = (2 * sg_ref[:, cols] - 1).astype(jnp.float32).astype(jnp.bfloat16)
        lhs = (x_ref[:, :, cols] * sign).reshape(groups * group_rows, HB)
        y_ref[:, cols] = jnp.dot(lhs, w_ref[...], preferred_element_type=jnp.float32)
    for k, o_ref in enumerate(out_refs):

        @pl.when(step == k)
        def _(o_ref=o_ref):
            coder = functools.partial(code_rows, y_ref, sh_ref, o_ref, group_rows, first_row)
            lax.fori_loop(0, groups * group_rows // 8, coder, 0)


def decoded_terms(grad_groups, signs, walsh, shifts, part, x_size):
    dests, _, part_rows, width = grad_groups.shape
    per_x = dests // x_size
    my_x = jnp.reshape(lax.axis_index("wx"), (1,)).astype(jnp.int32)
    tile = lambda i, mx, sh: ((mx[0] + i) % x_size, part, 0, 0)
    whole = lambda i, mx, sh: (0, 0)
    out_rows = per_x * part_rows
    return pl.pallas_call(
        functools.partial(code_kernel, part, x_size),
        grid_spec=pltpu.PrefetchScalarGridSpec(
            num_scalar_prefetch=2,
            grid=(x_size,),
            in_specs=[
                pl.BlockSpec((per_x, None, part_rows, width), tile),
                pl.BlockSpec((1, width), whole),
                pl.BlockSpec((HB, HB), whole),
            ],
            out_specs=[pl.BlockSpec((out_rows, width), whole) for _ in range(x_size)],
            scratch_shapes=[pltpu.VMEM((out_rows, width), jnp.float32)],
        ),
        out_shape=[jax.ShapeDtypeStruct((out_rows, width), jnp.bfloat16) for _ in range(x_size)],
        cost_estimate=pl.CostEstimate(
            flops=2 * dests * part_rows * width * HB + 8 * dests * part_rows * width,
            transcendentals=0,
            bytes_accessed=dests * part_rows * width * 4,
        ),
    )(my_x, shifts, grad_groups, signs, walsh)


def update_kernel(workers, p0_ref, p1_ref, f_ref, s_ref, w_ref, sg_ref, h_ref,
                  nf_ref, ns_ref, nw_ref, nb_ref, y_ref):
    half = p0_ref.shape[0]
    rows_all = 2 * half
    for part, p_ref in enumerate((p0_ref, p1_ref)):
        rows = slice(part * half, (part + 1) * half)
        mean_grad = p_ref[...] * (1.0 / workers)
        new_first = first_keep * f_ref[rows, :] + first_take * mean_grad
        new_second = second_keep * s_ref[rows, :] + second_take * mean_grad * mean_grad
        nf_ref[rows, :] = new_first
        ns_ref[rows, :] = new_second
        nb_ref[rows, :] = new_first / first_fix / (jnp.sqrt(new_second / second_fix) + adam_eps)
    stacked = jnp.concatenate([nb_ref[:, a * HB:(a + 1) * HB] for a in range(HA)], axis=0)
    high = stacked.astype(jnp.bfloat16)
    rest = stacked - high.astype(jnp.float32)
    mid = rest.astype(jnp.bfloat16)
    low = (rest - mid.astype(jnp.float32)).astype(jnp.bfloat16)
    walsh = h_ref[...]
    y_ref[...] = (
        jnp.dot(high, walsh, preferred_element_type=jnp.float32)
        + jnp.dot(mid, walsh, preferred_element_type=jnp.float32)
        + jnp.dot(low, walsh, preferred_element_type=jnp.float32)
    )
    for g in range(rows_all // 8):
        blocks = butterfly([y_ref[a * rows_all + g * 8:a * rows_all + g * 8 + 8, :] for a in range(HA)])
        for a in range(HA):
            cols = slice(a * HB, (a + 1) * HB)
            sign = (2 * sg_ref[:, cols] - 1).astype(jnp.float32)
            step = blocks[a] * (1.0 / math.sqrt(HA * HB)) * sign
            updated = w_ref[g * 8:g * 8 + 8, cols] - learn_rate * step
            nw_ref[g * 8:g * 8 + 8, cols] = updated
            nb_ref[g * 8:g * 8 + 8, cols] = updated


def adam_update(pieces, first_rows, second_rows, weight_rows, signs, walsh, workers):
    rows, width = first_rows.shape
    f32 = jax.ShapeDtypeStruct((rows, width), jnp.float32)
    nf, ns, nw, nb = pl.pallas_call(
        functools.partial(update_kernel, workers),
        out_shape=[f32, f32, f32, f32],
        scratch_shapes=[pltpu.VMEM((rows * HA, HB), jnp.float32)],
        cost_estimate=pl.CostEstimate(
            flops=6 * rows * width * HB, transcendentals=rows * width, bytes_accessed=rows * width * 32
        ),
    )(pieces[0], pieces[1], first_rows, second_rows, weight_rows, signs, walsh)
    return nf, ns, nw, nb


def send_along_x(terms, x_size):
    arrived = [terms[0]]
    for step in range(1, x_size):
        pairs = [(i, (i + step) % x_size) for i in range(x_size)]
        arrived.append(lax.ppermute(terms[step], "wx", pairs))
    return arrived


def sum_arrived(arrived):
    partial = arrived[0].astype(jnp.float32)
    for piece in arrived[1:]:
        partial = partial + piece.astype(jnp.float32)
    return partial


def select_pieces(slab_view, slot_lists, used_counts):
    gathered = jnp.take_along_axis(slab_view, slot_lists[:, :, None], axis=1)
    live_slots = lax.broadcasted_iota(jnp.int32, slot_lists.shape, 1) < used_counts[:, None]
    return jnp.where(live_slots[:, :, None], gathered, jnp.zeros((), jnp.bfloat16))


def per_device(grads, signs, shifts, first, second, weights, slots, counts):
    sign_vec = (2 * signs[0] - 1).astype(jnp.float32)
    grad_rows = grads[0, 0]
    blocks = first.shape[1]
    walsh = walsh_constant(HB)
    x_size = lax.axis_size("wx")
    dests = x_size * lax.axis_size("wz")
    workers = dests
    part_rows = blocks // PARTS
    grad_groups = grad_rows.reshape(dests, PARTS, part_rows, grad_rows.shape[-1])
    pieces = []
    terms = decoded_terms(grad_groups, signs, walsh, shifts, 0, x_size)
    arrived = send_along_x(terms, x_size)
    for part in range(1, PARTS + 1):
        if part < PARTS:
            terms = decoded_terms(grad_groups, signs, walsh, shifts, part, x_size)
            arrived, terms = lax.optimization_barrier((arrived, terms))
        partial = sum_arrived(arrived)
        pieces.append(lax.psum_scatter(partial, "wz", scatter_dimension=0, tiled=True))
        if part < PARTS:
            arrived = send_along_x(terms, x_size)
    new_first, new_second, new_weights, _ = adam_update(
        pieces, first[0], second[0], weights[0], signs, walsh, workers
    )
    owners = lax.axis_size("tensor")
    piece_width = new_weights.shape[1] // owners
    narrow = new_weights.astype(jnp.bfloat16).reshape(blocks, owners, piece_width)
    slab_view = jnp.transpose(narrow, (1, 0, 2))
    slot_lists = slots[0, 0]
    used_counts = counts[0, 0]
    chosen_pieces = select_pieces(slab_view, slot_lists, used_counts)
    arrived = lax.all_to_all(chosen_pieces, "tensor", split_axis=0, concat_axis=0, tiled=True)
    return (new_first[None], new_second[None], new_weights[None], arrived[None, None])


def solution(mesh):
    dp_size, tensor_size = mesh.devices.shape
    split_mesh = Mesh(
        mesh.devices.reshape(X_CHIPS, dp_size // X_CHIPS, tensor_size), WORKERS + ("tensor",)
    )
    return jax.shard_map(
        per_device,
        mesh=split_mesh,
        in_specs=(
            P(WORKERS, "tensor", None, None),
            P("tensor", None),
            P(WORKERS, "tensor", None),
            P("tensor", WORKERS, None),
            P("tensor", WORKERS, None),
            P("tensor", WORKERS, None),
            P(WORKERS, "tensor", None, None),
            P(WORKERS, "tensor", None),
        ),
        out_specs=(
            P("tensor", WORKERS, None),
            P("tensor", WORKERS, None),
            P("tensor", WORKERS, None),
            P(WORKERS, "tensor", None, None, None),
        ),
        check_vma=False,
    )
```

```python
import functools
import math

import jax
import numpy as np
import jax.numpy as jnp
from jax import lax
from jax.experimental import pallas as pl
from jax.experimental.pallas import tpu as pltpu
from jax.sharding import Mesh
from jax.sharding import PartitionSpec as P

HA = 32
HB = 128
ROW_TILE = 256
X_CHIPS = 4
PARTS = 2
WORKERS = ("wx", "wz")


first_keep = 0.9
first_take = 0.1
second_keep = 0.95
second_take = 0.05
first_fix = 1.0 - 0.9**10
second_fix = 1.0 - 0.95**10
adam_eps = 1e-08
learn_rate = 0.2


def walsh_table(table_order):
    positions = jnp.arange(table_order, dtype=jnp.int32)
    common_bits = jnp.bitwise_and(positions[:, None], positions[None, :])
    parity_sum = jnp.zeros((table_order, table_order), jnp.int32)
    for bit_level in range(max(table_order.bit_length() - 1, 1)):
        parity_sum = parity_sum + jnp.bitwise_and(jnp.right_shift(common_bits, bit_level), 1)
    return (1 - 2 * jnp.bitwise_and(parity_sum, 1)).astype(jnp.float32)


def rotate(flat_rows):
    count_rows = flat_rows.shape[0]
    cube_rows = flat_rows.reshape(count_rows, HA, HB)
    cube_rows = jnp.einsum(
        "rab,bc->rac", cube_rows, walsh_table(HB), precision=lax.Precision.HIGHEST
    )
    cube_rows = jnp.einsum(
        "ka,rac->rkc", walsh_table(HA), cube_rows, precision=lax.Precision.HIGHEST
    )
    return cube_rows.reshape(count_rows, HA * HB) / math.sqrt(HA * HB)


def half_power(shift_vals):
    unit_scale = jnp.ones(shift_vals.shape, jnp.float32)
    factor = 0.5
    for bit_level in range(5):
        chosen = jnp.bitwise_and(jnp.right_shift(shift_vals, bit_level), 1) == 1
        unit_scale = unit_scale * jnp.where(chosen, factor, 1.0).astype(jnp.float32)
        factor = factor * factor
    return unit_scale


def butterfly(blocks):
    blocks = list(blocks)
    span = 1
    while span < len(blocks):
        for start in range(0, len(blocks), 2 * span):
            for j in range(start, start + span):
                u, v = blocks[j], blocks[j + span]
                blocks[j], blocks[j + span] = u + v, u - v
        span *= 2
    return blocks


def exact_powers(shift_vals):
    up = jnp.ones(shift_vals.shape, jnp.float32)
    down = jnp.ones(shift_vals.shape, jnp.float32)
    factor = 2.0
    for bit_level in range(5):
        chosen = jnp.bitwise_and(jnp.right_shift(shift_vals, bit_level), 1) == 1
        up = up * jnp.where(chosen, factor, 1.0)
        down = down * jnp.where(chosen, 1.0 / factor, 1.0)
        factor = factor * factor
    return up, down


def walsh_constant(table_order):
    positions = np.arange(table_order)
    common_bits = np.bitwise_and(positions[:, None], positions[None, :])
    parity = np.zeros((table_order, table_order), np.int64)
    for bit_level in range(max(table_order.bit_length() - 1, 1)):
        parity = parity + np.right_shift(common_bits, bit_level) % 2
    return jnp.asarray((1 - 2 * (parity % 2)).astype(np.float32), dtype=jnp.bfloat16)


def code_rows(y_ref, sh_ref, o_ref, group_rows, first_row, g, carry):
    rows = pl.ds(pl.multiple_of(g * 8, 8), 8)
    dest = g // (group_rows // 8)
    within = (g % (group_rows // 8)) * 8
    blocks = butterfly([y_ref[rows, a * HB:(a + 1) * HB] for a in range(HA)])
    base = first_row(dest) + within
    row_ids = lax.broadcasted_iota(jnp.int32, (8, 1), 0)
    shift_col = jnp.zeros((8, 1), jnp.int32)
    for j in range(8):
        shift_col = jnp.where(row_ids == j, sh_ref[0, 0, base + j], shift_col)
    up, dn = exact_powers(shift_col)
    up = up * (1.0 / math.sqrt(HA * HB))
    dn = dn.astype(jnp.bfloat16)
    for a in range(HA):
        coded = jnp.clip(blocks[a] * up, -127.0, 127.0).astype(jnp.bfloat16)
        o_ref[rows, a * HB:(a + 1) * HB] = (coded * dn).astype(o_ref.dtype)
    return carry


def code_kernel(part, x_size, mx_ref, sh_ref, x_ref, sg_ref, w_ref, *refs):
    out_refs, y_ref = refs[:-1], refs[-1]
    step = pl.program_id(0)
    groups, group_rows, _ = x_ref.shape
    dest_rows = group_rows * PARTS
    first_dest = ((mx_ref[0] + step) % x_size) * groups
    first_row = lambda dest: (first_dest + dest) * dest_rows + part * group_rows
    for a in range(HA):
        cols = slice(a * HB, (a + 1) * HB)
        sign = (2 * sg_ref[:, cols] - 1).astype(jnp.float32).astype(jnp.bfloat16)
        lhs = (x_ref[:, :, cols] * sign).reshape(groups * group_rows, HB)
        y_ref[:, cols] = jnp.dot(lhs, w_ref[...], preferred_element_type=jnp.float32)
    for k, o_ref in enumerate(out_refs):

        @pl.when(step == k)
        def _(o_ref=o_ref):
            coder = functools.partial(code_rows, y_ref, sh_ref, o_ref, group_rows, first_row)
            lax.fori_loop(0, groups * group_rows // 8, coder, 0)


def decoded_terms(grad_groups, signs, walsh, shifts, part, x_size):
    dests, _, part_rows, width = grad_groups.shape
    per_x = dests // x_size
    my_x = jnp.reshape(lax.axis_index("wx"), (1,)).astype(jnp.int32)
    tile = lambda i, mx, sh: ((mx[0] + i) % x_size, part, 0, 0)
    whole = lambda i, mx, sh: (0, 0)
    out_rows = per_x * part_rows
    return pl.pallas_call(
        functools.partial(code_kernel, part, x_size),
        grid_spec=pltpu.PrefetchScalarGridSpec(
            num_scalar_prefetch=2,
            grid=(x_size,),
            in_specs=[
                pl.BlockSpec((per_x, None, part_rows, width), tile),
                pl.BlockSpec((1, width), whole),
                pl.BlockSpec((HB, HB), whole),
            ],
            out_specs=[pl.BlockSpec((out_rows, width), whole) for _ in range(x_size)],
            scratch_shapes=[pltpu.VMEM((out_rows, width), jnp.float32)],
        ),
        out_shape=[jax.ShapeDtypeStruct((out_rows, width), jnp.bfloat16) for _ in range(x_size)],
        cost_estimate=pl.CostEstimate(
            flops=2 * dests * part_rows * width * HB + 8 * dests * part_rows * width,
            transcendentals=0,
            bytes_accessed=dests * part_rows * width * 4,
        ),
    )(my_x, shifts, grad_groups, signs, walsh)


def update_kernel(workers, p0_ref, p1_ref, f_ref, s_ref, w_ref, sg_ref, h_ref,
                  nf_ref, ns_ref, nw_ref, nb_ref, sd_ref, y_ref):
    half = p0_ref.shape[0]
    rows_all = 2 * half
    for part, p_ref in enumerate((p0_ref, p1_ref)):
        rows = slice(part * half, (part + 1) * half)
        mean_grad = p_ref[...] * (1.0 / workers)
        new_first = first_keep * f_ref[rows, :] + first_take * mean_grad
        new_second = second_keep * s_ref[rows, :] + second_take * mean_grad * mean_grad
        nf_ref[rows, :] = new_first
        ns_ref[rows, :] = new_second
        sd_ref[rows, :] = new_first / first_fix / (jnp.sqrt(new_second / second_fix) + adam_eps)
    stacked = jnp.concatenate([sd_ref[:, a * HB:(a + 1) * HB] for a in range(HA)], axis=0)
    high = stacked.astype(jnp.bfloat16)
    rest = stacked - high.astype(jnp.float32)
    mid = rest.astype(jnp.bfloat16)
    low = (rest - mid.astype(jnp.float32)).astype(jnp.bfloat16)
    walsh = h_ref[...]
    y_ref[...] = (
        jnp.dot(high, walsh, preferred_element_type=jnp.float32)
        + jnp.dot(mid, walsh, preferred_element_type=jnp.float32)
        + jnp.dot(low, walsh, preferred_element_type=jnp.float32)
    )
    for g in range(rows_all // 8):
        blocks = butterfly([y_ref[a * rows_all + g * 8:a * rows_all + g * 8 + 8, :] for a in range(HA)])
        for a in range(HA):
            cols = slice(a * HB, (a + 1) * HB)
            sign = (2 * sg_ref[:, cols] - 1).astype(jnp.float32)
            step = blocks[a] * (1.0 / math.sqrt(HA * HB)) * sign
            updated = w_ref[g * 8:g * 8 + 8, cols] - learn_rate * step
            nw_ref[g * 8:g * 8 + 8, cols] = updated
            nb_ref[g * 8:g * 8 + 8, cols] = updated.astype(nb_ref.dtype)


def adam_update(pieces, first_rows, second_rows, weight_rows, signs, walsh, workers):
    rows, width = first_rows.shape
    f32 = jax.ShapeDtypeStruct((rows, width), jnp.float32)
    nf, ns, nw, nb = pl.pallas_call(
        functools.partial(update_kernel, workers),
        out_shape=[f32, f32, f32, jax.ShapeDtypeStruct((rows, width), jnp.bfloat16)],
        scratch_shapes=[pltpu.VMEM((rows, width), jnp.float32), pltpu.VMEM((rows * HA, HB), jnp.float32)],
        cost_estimate=pl.CostEstimate(
            flops=6 * rows * width * HB, transcendentals=rows * width, bytes_accessed=rows * width * 32
        ),
    )(pieces[0], pieces[1], first_rows, second_rows, weight_rows, signs, walsh)
    return nf, ns, nw, nb


def send_along_x(terms, x_size):
    arrived = [terms[0]]
    for step in range(1, x_size):
        pairs = [(i, (i + step) % x_size) for i in range(x_size)]
        arrived.append(lax.ppermute(terms[step], "wx", pairs))
    return arrived


def sum_arrived(arrived):
    partial = arrived[0].astype(jnp.float32)
    for piece in arrived[1:]:
        partial = partial + piece.astype(jnp.float32)
    return partial


def select_pieces(slab_view, slot_lists, used_counts):
    gathered = jnp.take_along_axis(slab_view, slot_lists[:, :, None], axis=1)
    live_slots = lax.broadcasted_iota(jnp.int32, slot_lists.shape, 1) < used_counts[:, None]
    return jnp.where(live_slots[:, :, None], gathered, jnp.zeros((), jnp.bfloat16))


def per_device(grads, signs, shifts, first, second, weights, slots, counts):
    sign_vec = (2 * signs[0] - 1).astype(jnp.float32)
    grad_rows = grads[0, 0]
    blocks = first.shape[1]
    walsh = walsh_constant(HB)
    x_size = lax.axis_size("wx")
    dests = x_size * lax.axis_size("wz")
    workers = dests
    part_rows = blocks // PARTS
    grad_groups = grad_rows.reshape(dests, PARTS, part_rows, grad_rows.shape[-1])
    pieces = []
    terms = decoded_terms(grad_groups, signs, walsh, shifts, 0, x_size)
    arrived = send_along_x(terms, x_size)
    for part in range(1, PARTS + 1):
        if part < PARTS:
            terms = decoded_terms(grad_groups, signs, walsh, shifts, part, x_size)
            arrived, terms = lax.optimization_barrier((arrived, terms))
        partial = sum_arrived(arrived)
        pieces.append(lax.psum_scatter(partial, "wz", scatter_dimension=0, tiled=True))
        if part < PARTS:
            arrived = send_along_x(terms, x_size)
    new_first, new_second, new_weights, narrow_weights = adam_update(
        pieces, first[0], second[0], weights[0], signs, walsh, workers
    )
    owners = lax.axis_size("tensor")
    piece_width = new_weights.shape[1] // owners
    narrow = narrow_weights.reshape(blocks, owners, piece_width)
    slab_view = jnp.transpose(narrow, (1, 0, 2))
    slot_lists = slots[0, 0]
    used_counts = counts[0, 0]
    chosen_pieces = select_pieces(slab_view, slot_lists, used_counts)
    arrived = lax.all_to_all(chosen_pieces, "tensor", split_axis=0, concat_axis=0, tiled=True)
    return (new_first[None], new_second[None], new_weights[None], arrived[None, None])


def solution(mesh):
    dp_size, tensor_size = mesh.devices.shape
    split_mesh = Mesh(
        mesh.devices.reshape(X_CHIPS, dp_size // X_CHIPS, tensor_size), WORKERS + ("tensor",)
    )
    return jax.shard_map(
        per_device,
        mesh=split_mesh,
        in_specs=(
            P(WORKERS, "tensor", None, None),
            P("tensor", None),
            P(WORKERS, "tensor", None),
            P("tensor", WORKERS, None),
            P("tensor", WORKERS, None),
            P("tensor", WORKERS, None),
            P(WORKERS, "tensor", None, None),
            P(WORKERS, "tensor", None),
        ),
        out_specs=(
            P("tensor", WORKERS, None),
            P("tensor", WORKERS, None),
            P("tensor", WORKERS, None),
            P(WORKERS, "tensor", None, None, None),
        ),
        check_vma=False,
    )
```

```python
import functools
import math

import jax
import numpy as np
import jax.numpy as jnp
from jax import lax
from jax.experimental import pallas as pl
from jax.experimental.pallas import tpu as pltpu
from jax.sharding import Mesh
from jax.sharding import PartitionSpec as P

HA = 32
HB = 128
ROW_TILE = 256
X_CHIPS = 4
PARTS = 2
WORKERS = ("wx", "wz")


first_keep = 0.9
first_take = 0.1
second_keep = 0.95
second_take = 0.05
first_fix = 1.0 - 0.9**10
second_fix = 1.0 - 0.95**10
adam_eps = 1e-08
learn_rate = 0.2


def walsh_table(table_order):
    positions = jnp.arange(table_order, dtype=jnp.int32)
    common_bits = jnp.bitwise_and(positions[:, None], positions[None, :])
    parity_sum = jnp.zeros((table_order, table_order), jnp.int32)
    for bit_level in range(max(table_order.bit_length() - 1, 1)):
        parity_sum = parity_sum + jnp.bitwise_and(jnp.right_shift(common_bits, bit_level), 1)
    return (1 - 2 * jnp.bitwise_and(parity_sum, 1)).astype(jnp.float32)


def rotate(flat_rows):
    count_rows = flat_rows.shape[0]
    cube_rows = flat_rows.reshape(count_rows, HA, HB)
    cube_rows = jnp.einsum(
        "rab,bc->rac", cube_rows, walsh_table(HB), precision=lax.Precision.HIGHEST
    )
    cube_rows = jnp.einsum(
        "ka,rac->rkc", walsh_table(HA), cube_rows, precision=lax.Precision.HIGHEST
    )
    return cube_rows.reshape(count_rows, HA * HB) / math.sqrt(HA * HB)


def half_power(shift_vals):
    unit_scale = jnp.ones(shift_vals.shape, jnp.float32)
    factor = 0.5
    for bit_level in range(5):
        chosen = jnp.bitwise_and(jnp.right_shift(shift_vals, bit_level), 1) == 1
        unit_scale = unit_scale * jnp.where(chosen, factor, 1.0).astype(jnp.float32)
        factor = factor * factor
    return unit_scale


def butterfly(blocks):
    blocks = list(blocks)
    span = 1
    while span < len(blocks):
        for start in range(0, len(blocks), 2 * span):
            for j in range(start, start + span):
                u, v = blocks[j], blocks[j + span]
                blocks[j], blocks[j + span] = u + v, u - v
        span *= 2
    return blocks


def exact_powers(shift_vals):
    up = jnp.ones(shift_vals.shape, jnp.float32)
    down = jnp.ones(shift_vals.shape, jnp.float32)
    factor = 2.0
    for bit_level in range(5):
        chosen = jnp.bitwise_and(jnp.right_shift(shift_vals, bit_level), 1) == 1
        up = up * jnp.where(chosen, factor, 1.0)
        down = down * jnp.where(chosen, 1.0 / factor, 1.0)
        factor = factor * factor
    return up, down


def walsh_constant(table_order):
    positions = np.arange(table_order)
    common_bits = np.bitwise_and(positions[:, None], positions[None, :])
    parity = np.zeros((table_order, table_order), np.int64)
    for bit_level in range(max(table_order.bit_length() - 1, 1)):
        parity = parity + np.right_shift(common_bits, bit_level) % 2
    return jnp.asarray((1 - 2 * (parity % 2)).astype(np.float32), dtype=jnp.bfloat16)


def code_rows(y_ref, sh_ref, o_ref, group_rows, first_row, g, carry):
    rows = pl.ds(pl.multiple_of(g * 8, 8), 8)
    dest = g // (group_rows // 8)
    within = (g % (group_rows // 8)) * 8
    blocks = butterfly([y_ref[rows, a * HB:(a + 1) * HB] for a in range(HA)])
    base = first_row(dest) + within
    row_ids = lax.broadcasted_iota(jnp.int32, (8, 1), 0)
    shift_col = jnp.zeros((8, 1), jnp.int32)
    for j in range(8):
        shift_col = jnp.where(row_ids == j, sh_ref[0, 0, base + j], shift_col)
    up, dn = exact_powers(shift_col)
    up = up * (1.0 / math.sqrt(HA * HB))
    dn = dn.astype(jnp.bfloat16)
    for a in range(HA):
        coded = jnp.clip(blocks[a] * up, -127.0, 127.0).astype(jnp.bfloat16)
        o_ref[rows, a * HB:(a + 1) * HB] = (coded * dn).astype(o_ref.dtype)
    return carry


def code_kernel(part, x_size, mx_ref, sh_ref, x_ref, sg_ref, w_ref, *refs):
    out_refs, y_ref = refs[:-1], refs[-1]
    step = pl.program_id(0)
    groups, group_rows, _ = x_ref.shape
    dest_rows = group_rows * PARTS
    first_dest = ((mx_ref[0] + step) % x_size) * groups
    first_row = lambda dest: (first_dest + dest) * dest_rows + part * group_rows
    for a in range(HA):
        cols = slice(a * HB, (a + 1) * HB)
        sign = (2 * sg_ref[:, cols] - 1).astype(jnp.float32).astype(jnp.bfloat16)
        lhs = (x_ref[:, :, cols] * sign).reshape(groups * group_rows, HB)
        y_ref[:, cols] = jnp.dot(lhs, w_ref[...], preferred_element_type=jnp.float32)
    for k, o_ref in enumerate(out_refs):

        @pl.when(step == k)
        def _(o_ref=o_ref):
            coder = functools.partial(code_rows, y_ref, sh_ref, o_ref, group_rows, first_row)
            lax.fori_loop(0, groups * group_rows // 8, coder, 0)


def decoded_terms(grad_groups, signs, walsh, shifts, part, x_size):
    dests, _, part_rows, width = grad_groups.shape
    per_x = dests // x_size
    my_x = jnp.reshape(lax.axis_index("wx"), (1,)).astype(jnp.int32)
    tile = lambda i, mx, sh: ((mx[0] + i) % x_size, part, 0, 0)
    whole = lambda i, mx, sh: (0, 0)
    out_rows = per_x * part_rows
    return pl.pallas_call(
        functools.partial(code_kernel, part, x_size),
        grid_spec=pltpu.PrefetchScalarGridSpec(
            num_scalar_prefetch=2,
            grid=(x_size,),
            in_specs=[
                pl.BlockSpec((per_x, None, part_rows, width), tile),
                pl.BlockSpec((1, width), whole),
                pl.BlockSpec((HB, HB), whole),
            ],
            out_specs=[pl.BlockSpec((out_rows, width), whole) for _ in range(x_size)],
            scratch_shapes=[pltpu.VMEM((out_rows, width), jnp.float32)],
        ),
        out_shape=[jax.ShapeDtypeStruct((out_rows, width), jnp.bfloat16) for _ in range(x_size)],
        cost_estimate=pl.CostEstimate(
            flops=2 * dests * part_rows * width * HB + 8 * dests * part_rows * width,
            transcendentals=0,
            bytes_accessed=dests * part_rows * width * 4,
        ),
    )(my_x, shifts, grad_groups, signs, walsh)


def update_kernel(workers, p0_ref, p1_ref, f_ref, s_ref, w_ref, sg_ref, h_ref,
                  nf_ref, ns_ref, nw_ref, nb_ref, sd_ref, y_ref):
    half = p0_ref.shape[0]
    rows_all = 2 * half
    for part, p_ref in enumerate((p0_ref, p1_ref)):
        rows = slice(part * half, (part + 1) * half)
        mean_grad = p_ref[...] * (1.0 / workers)
        new_first = first_keep * f_ref[rows, :] + first_take * mean_grad
        new_second = second_keep * s_ref[rows, :] + second_take * mean_grad * mean_grad
        nf_ref[rows, :] = new_first
        ns_ref[rows, :] = new_second
        sd_ref[rows, :] = new_first / first_fix / (jnp.sqrt(new_second / second_fix) + adam_eps)
    stacked = jnp.concatenate([sd_ref[:, a * HB:(a + 1) * HB] for a in range(HA)], axis=0)
    high = stacked.astype(jnp.bfloat16)
    rest = stacked - high.astype(jnp.float32)
    mid = rest.astype(jnp.bfloat16)
    low = (rest - mid.astype(jnp.float32)).astype(jnp.bfloat16)
    walsh = h_ref[...]
    y_ref[...] = (
        jnp.dot(high, walsh, preferred_element_type=jnp.float32)
        + jnp.dot(mid, walsh, preferred_element_type=jnp.float32)
        + jnp.dot(low, walsh, preferred_element_type=jnp.float32)
    )
    for g in range(rows_all // 8):
        blocks = butterfly([y_ref[a * rows_all + g * 8:a * rows_all + g * 8 + 8, :] for a in range(HA)])
        for a in range(HA):
            cols = slice(a * HB, (a + 1) * HB)
            sign = (2 * sg_ref[:, cols] - 1).astype(jnp.float32)
            step = blocks[a] * (1.0 / math.sqrt(HA * HB)) * sign
            updated = w_ref[g * 8:g * 8 + 8, cols] - learn_rate * step
            nw_ref[g * 8:g * 8 + 8, cols] = updated
            per_owner = nb_ref.shape[2] // HB
            owner_cols = slice((a % per_owner) * HB, (a % per_owner + 1) * HB)
            nb_ref[a // per_owner, g * 8:g * 8 + 8, owner_cols] = updated.astype(nb_ref.dtype)


def adam_update(pieces, first_rows, second_rows, weight_rows, signs, walsh, workers, owners):
    rows, width = first_rows.shape
    f32 = jax.ShapeDtypeStruct((rows, width), jnp.float32)
    nf, ns, nw, nb = pl.pallas_call(
        functools.partial(update_kernel, workers),
        out_shape=[f32, f32, f32, jax.ShapeDtypeStruct((owners, rows, width // owners), jnp.bfloat16)],
        scratch_shapes=[pltpu.VMEM((rows, width), jnp.float32), pltpu.VMEM((rows * HA, HB), jnp.float32)],
        cost_estimate=pl.CostEstimate(
            flops=6 * rows * width * HB, transcendentals=rows * width, bytes_accessed=rows * width * 32
        ),
    )(pieces[0], pieces[1], first_rows, second_rows, weight_rows, signs, walsh)
    return nf, ns, nw, nb


def send_along_x(terms, x_size):
    arrived = [terms[0]]
    for step in range(1, x_size):
        pairs = [(i, (i + step) % x_size) for i in range(x_size)]
        arrived.append(lax.ppermute(terms[step], "wx", pairs))
    return arrived


def sum_arrived(arrived):
    partial = arrived[0].astype(jnp.float32)
    for piece in arrived[1:]:
        partial = partial + piece.astype(jnp.float32)
    return partial


def select_pieces(slab_view, slot_lists, used_counts):
    gathered = jnp.take_along_axis(slab_view, slot_lists[:, :, None], axis=1)
    live_slots = lax.broadcasted_iota(jnp.int32, slot_lists.shape, 1) < used_counts[:, None]
    return jnp.where(live_slots[:, :, None], gathered, jnp.zeros((), jnp.bfloat16))


def per_device(grads, signs, shifts, first, second, weights, slots, counts):
    sign_vec = (2 * signs[0] - 1).astype(jnp.float32)
    grad_rows = grads[0, 0]
    blocks = first.shape[1]
    walsh = walsh_constant(HB)
    x_size = lax.axis_size("wx")
    dests = x_size * lax.axis_size("wz")
    workers = dests
    part_rows = blocks // PARTS
    grad_groups = grad_rows.reshape(dests, PARTS, part_rows, grad_rows.shape[-1])
    pieces = []
    terms = decoded_terms(grad_groups, signs, walsh, shifts, 0, x_size)
    arrived = send_along_x(terms, x_size)
    for part in range(1, PARTS + 1):
        if part < PARTS:
            terms = decoded_terms(grad_groups, signs, walsh, shifts, part, x_size)
            arrived, terms = lax.optimization_barrier((arrived, terms))
        partial = sum_arrived(arrived)
        pieces.append(lax.psum_scatter(partial, "wz", scatter_dimension=0, tiled=True))
        if part < PARTS:
            arrived = send_along_x(terms, x_size)
    owners = lax.axis_size("tensor")
    new_first, new_second, new_weights, slab_view = adam_update(
        pieces, first[0], second[0], weights[0], signs, walsh, workers, owners
    )
    slot_lists = slots[0, 0]
    used_counts = counts[0, 0]
    chosen_pieces = select_pieces(slab_view, slot_lists, used_counts)
    arrived = lax.all_to_all(chosen_pieces, "tensor", split_axis=0, concat_axis=0, tiled=True)
    return (new_first[None], new_second[None], new_weights[None], arrived[None, None])


def solution(mesh):
    dp_size, tensor_size = mesh.devices.shape
    split_mesh = Mesh(
        mesh.devices.reshape(X_CHIPS, dp_size // X_CHIPS, tensor_size), WORKERS + ("tensor",)
    )
    return jax.shard_map(
        per_device,
        mesh=split_mesh,
        in_specs=(
            P(WORKERS, "tensor", None, None),
            P("tensor", None),
            P(WORKERS, "tensor", None),
            P("tensor", WORKERS, None),
            P("tensor", WORKERS, None),
            P("tensor", WORKERS, None),
            P(WORKERS, "tensor", None, None),
            P(WORKERS, "tensor", None),
        ),
        out_specs=(
            P("tensor", WORKERS, None),
            P("tensor", WORKERS, None),
            P("tensor", WORKERS, None),
            P(WORKERS, "tensor", None, None, None),
        ),
        check_vma=False,
    )
```

```python
import functools
import math

import jax
import numpy as np
import jax.numpy as jnp
from jax import lax
from jax.experimental import pallas as pl
from jax.experimental.pallas import tpu as pltpu
from jax.sharding import Mesh
from jax.sharding import PartitionSpec as P

HA = 32
HB = 128
ROW_TILE = 256
X_CHIPS = 4
PARTS = 2
WORKERS = ("wx", "wz")


first_keep = 0.9
first_take = 0.1
second_keep = 0.95
second_take = 0.05
first_fix = 1.0 - 0.9**10
second_fix = 1.0 - 0.95**10
adam_eps = 1e-08
learn_rate = 0.2


def walsh_table(table_order):
    positions = jnp.arange(table_order, dtype=jnp.int32)
    common_bits = jnp.bitwise_and(positions[:, None], positions[None, :])
    parity_sum = jnp.zeros((table_order, table_order), jnp.int32)
    for bit_level in range(max(table_order.bit_length() - 1, 1)):
        parity_sum = parity_sum + jnp.bitwise_and(jnp.right_shift(common_bits, bit_level), 1)
    return (1 - 2 * jnp.bitwise_and(parity_sum, 1)).astype(jnp.float32)


def rotate(flat_rows):
    count_rows = flat_rows.shape[0]
    cube_rows = flat_rows.reshape(count_rows, HA, HB)
    cube_rows = jnp.einsum(
        "rab,bc->rac", cube_rows, walsh_table(HB), precision=lax.Precision.HIGHEST
    )
    cube_rows = jnp.einsum(
        "ka,rac->rkc", walsh_table(HA), cube_rows, precision=lax.Precision.HIGHEST
    )
    return cube_rows.reshape(count_rows, HA * HB) / math.sqrt(HA * HB)


def half_power(shift_vals):
    unit_scale = jnp.ones(shift_vals.shape, jnp.float32)
    factor = 0.5
    for bit_level in range(5):
        chosen = jnp.bitwise_and(jnp.right_shift(shift_vals, bit_level), 1) == 1
        unit_scale = unit_scale * jnp.where(chosen, factor, 1.0).astype(jnp.float32)
        factor = factor * factor
    return unit_scale


def butterfly(blocks):
    blocks = list(blocks)
    span = 1
    while span < len(blocks):
        for start in range(0, len(blocks), 2 * span):
            for j in range(start, start + span):
                u, v = blocks[j], blocks[j + span]
                blocks[j], blocks[j + span] = u + v, u - v
        span *= 2
    return blocks


def exact_powers(shift_vals):
    up = jnp.ones(shift_vals.shape, jnp.float32)
    down = jnp.ones(shift_vals.shape, jnp.float32)
    factor = 2.0
    for bit_level in range(5):
        chosen = jnp.bitwise_and(jnp.right_shift(shift_vals, bit_level), 1) == 1
        up = up * jnp.where(chosen, factor, 1.0)
        down = down * jnp.where(chosen, 1.0 / factor, 1.0)
        factor = factor * factor
    return up, down


def walsh_constant(table_order):
    positions = np.arange(table_order)
    common_bits = np.bitwise_and(positions[:, None], positions[None, :])
    parity = np.zeros((table_order, table_order), np.int64)
    for bit_level in range(max(table_order.bit_length() - 1, 1)):
        parity = parity + np.right_shift(common_bits, bit_level) % 2
    return jnp.asarray((1 - 2 * (parity % 2)).astype(np.float32), dtype=jnp.bfloat16)


def code_rows(y_ref, sh_ref, o_ref, group_rows, first_row, g, carry):
    rows = pl.ds(pl.multiple_of(g * 8, 8), 8)
    dest = g // (group_rows // 8)
    within = (g % (group_rows // 8)) * 8
    blocks = butterfly([y_ref[rows, a * HB:(a + 1) * HB] for a in range(HA)])
    base = first_row(dest) + within
    row_ids = lax.broadcasted_iota(jnp.int32, (8, 1), 0)
    shift_col = jnp.zeros((8, 1), jnp.int32)
    for j in range(8):
        shift_col = jnp.where(row_ids == j, sh_ref[0, 0, base + j], shift_col)
    up, dn = exact_powers(shift_col)
    up = up * (1.0 / math.sqrt(HA * HB))
    dn = dn.astype(jnp.bfloat16)
    for a in range(HA):
        coded = jnp.clip(blocks[a] * up, -127.0, 127.0).astype(jnp.bfloat16)
        o_ref[rows, a * HB:(a + 1) * HB] = (coded * dn).astype(o_ref.dtype)
    return carry


def code_kernel(part, x_size, mx_ref, sh_ref, x_ref, sg_ref, w_ref, *refs):
    out_refs, y_ref = refs[:-1], refs[-1]
    step = pl.program_id(0)
    groups, group_rows, _ = x_ref.shape
    dest_rows = group_rows * PARTS
    first_dest = ((mx_ref[0] + step) % x_size) * groups
    first_row = lambda dest: (first_dest + dest) * dest_rows + part * group_rows
    for a in range(HA):
        cols = slice(a * HB, (a + 1) * HB)
        sign = (2 * sg_ref[:, cols] - 1).astype(jnp.float32).astype(jnp.bfloat16)
        lhs = (x_ref[:, :, cols] * sign).reshape(groups * group_rows, HB)
        y_ref[:, cols] = jnp.dot(lhs, w_ref[...], preferred_element_type=jnp.float32)
    for k, o_ref in enumerate(out_refs):

        @pl.when(step == k)
        def _(o_ref=o_ref):
            coder = functools.partial(code_rows, y_ref, sh_ref, o_ref, group_rows, first_row)
            lax.fori_loop(0, groups * group_rows // 8, coder, 0)


def decoded_terms(grad_groups, signs, walsh, shifts, part, x_size):
    dests, _, part_rows, width = grad_groups.shape
    per_x = dests // x_size
    my_x = jnp.reshape(lax.axis_index("wx"), (1,)).astype(jnp.int32)
    tile = lambda i, mx, sh: ((mx[0] + i) % x_size, part, 0, 0)
    whole = lambda i, mx, sh: (0, 0)
    out_rows = per_x * part_rows
    return pl.pallas_call(
        functools.partial(code_kernel, part, x_size),
        grid_spec=pltpu.PrefetchScalarGridSpec(
            num_scalar_prefetch=2,
            grid=(x_size,),
            in_specs=[
                pl.BlockSpec((per_x, None, part_rows, width), tile),
                pl.BlockSpec((1, width), whole),
                pl.BlockSpec((HB, HB), whole),
            ],
            out_specs=[pl.BlockSpec((out_rows, width), whole) for _ in range(x_size)],
            scratch_shapes=[pltpu.VMEM((out_rows, width), jnp.float32)],
        ),
        out_shape=[jax.ShapeDtypeStruct((out_rows, width), jnp.bfloat16) for _ in range(x_size)],
        cost_estimate=pl.CostEstimate(
            flops=2 * dests * part_rows * width * HB + 8 * dests * part_rows * width,
            transcendentals=0,
            bytes_accessed=dests * part_rows * width * 4,
        ),
    )(my_x, shifts, grad_groups, signs, walsh)


def update_kernel(workers, p0_ref, p1_ref, f_ref, s_ref, w_ref, sg_ref, h_ref, sl_ref, ct_ref,
                  nf_ref, ns_ref, nw_ref, ch_ref, sd_ref, y_ref):
    half = p0_ref.shape[0]
    rows_all = 2 * half
    for part, p_ref in enumerate((p0_ref, p1_ref)):
        rows = slice(part * half, (part + 1) * half)
        mean_grad = p_ref[...] * (1.0 / workers)
        new_first = first_keep * f_ref[rows, :] + first_take * mean_grad
        new_second = second_keep * s_ref[rows, :] + second_take * mean_grad * mean_grad
        nf_ref[rows, :] = new_first
        ns_ref[rows, :] = new_second
        sd_ref[rows, :] = new_first / first_fix / (jnp.sqrt(new_second / second_fix) + adam_eps)
    stacked = jnp.concatenate([sd_ref[:, a * HB:(a + 1) * HB] for a in range(HA)], axis=0)
    high = stacked.astype(jnp.bfloat16)
    rest = stacked - high.astype(jnp.float32)
    mid = rest.astype(jnp.bfloat16)
    low = (rest - mid.astype(jnp.float32)).astype(jnp.bfloat16)
    walsh = h_ref[...]
    y_ref[...] = (
        jnp.dot(high, walsh, preferred_element_type=jnp.float32)
        + jnp.dot(mid, walsh, preferred_element_type=jnp.float32)
        + jnp.dot(low, walsh, preferred_element_type=jnp.float32)
    )
    for g in range(rows_all // 8):
        blocks = butterfly([y_ref[a * rows_all + g * 8:a * rows_all + g * 8 + 8, :] for a in range(HA)])
        for a in range(HA):
            cols = slice(a * HB, (a + 1) * HB)
            sign = (2 * sg_ref[:, cols] - 1).astype(jnp.float32)
            step = blocks[a] * (1.0 / math.sqrt(HA * HB)) * sign
            updated = w_ref[g * 8:g * 8 + 8, cols] - learn_rate * step
            nw_ref[g * 8:g * 8 + 8, cols] = updated
    owners, slots_per_list, piece_width = ch_ref.shape
    for owner in range(owners):
        used = ct_ref[0, 0, owner]
        owner_cols = slice(owner * piece_width, (owner + 1) * piece_width)
        for slot in range(slots_per_list):
            piece = nw_ref[pl.ds(sl_ref[0, 0, owner, slot], 1), owner_cols]
            ch_ref[owner, slot:slot + 1, :] = jnp.where(slot < used, piece, 0.0)


def adam_update(pieces, first_rows, second_rows, weight_rows, signs, walsh, workers, slots, counts):
    rows, width = first_rows.shape
    owners, cap = slots.shape[2], slots.shape[3]
    f32 = jax.ShapeDtypeStruct((rows, width), jnp.float32)
    vmem = pl.BlockSpec(memory_space=pltpu.VMEM)
    smem = pl.BlockSpec(memory_space=pltpu.SMEM)
    return pl.pallas_call(
        functools.partial(update_kernel, workers),
        in_specs=[vmem] * 7 + [smem, smem],
        out_specs=[vmem] * 4,
        out_shape=[f32, f32, f32, jax.ShapeDtypeStruct((owners, cap, width // owners), jnp.float32)],
        scratch_shapes=[pltpu.VMEM((rows, width), jnp.float32), pltpu.VMEM((rows * HA, HB), jnp.float32)],
        cost_estimate=pl.CostEstimate(
            flops=6 * rows * width * HB, transcendentals=rows * width, bytes_accessed=rows * width * 32
        ),
    )(pieces[0], pieces[1], first_rows, second_rows, weight_rows, signs, walsh, slots, counts)


def send_along_x(terms, x_size):
    arrived = [terms[0]]
    for step in range(1, x_size):
        pairs = [(i, (i + step) % x_size) for i in range(x_size)]
        arrived.append(lax.ppermute(terms[step], "wx", pairs))
    return arrived


def sum_arrived(arrived):
    partial = arrived[0].astype(jnp.float32)
    for piece in arrived[1:]:
        partial = partial + piece.astype(jnp.float32)
    return partial


def select_pieces(slab_view, slot_lists, used_counts):
    gathered = jnp.take_along_axis(slab_view, slot_lists[:, :, None], axis=1)
    live_slots = lax.broadcasted_iota(jnp.int32, slot_lists.shape, 1) < used_counts[:, None]
    return jnp.where(live_slots[:, :, None], gathered, jnp.zeros((), jnp.bfloat16))


def per_device(grads, signs, shifts, first, second, weights, slots, counts):
    sign_vec = (2 * signs[0] - 1).astype(jnp.float32)
    grad_rows = grads[0, 0]
    blocks = first.shape[1]
    walsh = walsh_constant(HB)
    x_size = lax.axis_size("wx")
    dests = x_size * lax.axis_size("wz")
    workers = dests
    part_rows = blocks // PARTS
    grad_groups = grad_rows.reshape(dests, PARTS, part_rows, grad_rows.shape[-1])
    pieces = []
    terms = decoded_terms(grad_groups, signs, walsh, shifts, 0, x_size)
    arrived = send_along_x(terms, x_size)
    for part in range(1, PARTS + 1):
        if part < PARTS:
            terms = decoded_terms(grad_groups, signs, walsh, shifts, part, x_size)
            arrived, terms = lax.optimization_barrier((arrived, terms))
        partial = sum_arrived(arrived)
        pieces.append(lax.psum_scatter(partial, "wz", scatter_dimension=0, tiled=True))
        if part < PARTS:
            arrived = send_along_x(terms, x_size)
    new_first, new_second, new_weights, chosen_pieces = adam_update(
        pieces, first[0], second[0], weights[0], signs, walsh, workers, slots, counts
    )
    chosen_pieces = chosen_pieces.astype(jnp.bfloat16)
    arrived = lax.all_to_all(chosen_pieces, "tensor", split_axis=0, concat_axis=0, tiled=True)
    return (new_first[None], new_second[None], new_weights[None], arrived[None, None])


def solution(mesh):
    dp_size, tensor_size = mesh.devices.shape
    split_mesh = Mesh(
        mesh.devices.reshape(X_CHIPS, dp_size // X_CHIPS, tensor_size), WORKERS + ("tensor",)
    )
    return jax.shard_map(
        per_device,
        mesh=split_mesh,
        in_specs=(
            P(WORKERS, "tensor", None, None),
            P("tensor", None),
            P(WORKERS, "tensor", None),
            P("tensor", WORKERS, None),
            P("tensor", WORKERS, None),
            P("tensor", WORKERS, None),
            P(WORKERS, "tensor", None, None),
            P(WORKERS, "tensor", None),
        ),
        out_specs=(
            P("tensor", WORKERS, None),
            P("tensor", WORKERS, None),
            P("tensor", WORKERS, None),
            P(WORKERS, "tensor", None, None, None),
        ),
        check_vma=False,
    )
```

```python
import functools
import math

import jax
import numpy as np
import jax.numpy as jnp
from jax import lax
from jax.experimental import pallas as pl
from jax.experimental.pallas import tpu as pltpu
from jax.sharding import Mesh
from jax.sharding import PartitionSpec as P

HA = 32
HB = 128
ROW_TILE = 256
X_CHIPS = 4
PARTS = 2
WORKERS = ("wx", "wz")


first_keep = 0.9
first_take = 0.1
second_keep = 0.95
second_take = 0.05
first_fix = 1.0 - 0.9**10
second_fix = 1.0 - 0.95**10
adam_eps = 1e-08
learn_rate = 0.2


def walsh_table(table_order):
    positions = jnp.arange(table_order, dtype=jnp.int32)
    common_bits = jnp.bitwise_and(positions[:, None], positions[None, :])
    parity_sum = jnp.zeros((table_order, table_order), jnp.int32)
    for bit_level in range(max(table_order.bit_length() - 1, 1)):
        parity_sum = parity_sum + jnp.bitwise_and(jnp.right_shift(common_bits, bit_level), 1)
    return (1 - 2 * jnp.bitwise_and(parity_sum, 1)).astype(jnp.float32)


def rotate(flat_rows):
    count_rows = flat_rows.shape[0]
    cube_rows = flat_rows.reshape(count_rows, HA, HB)
    cube_rows = jnp.einsum(
        "rab,bc->rac", cube_rows, walsh_table(HB), precision=lax.Precision.HIGHEST
    )
    cube_rows = jnp.einsum(
        "ka,rac->rkc", walsh_table(HA), cube_rows, precision=lax.Precision.HIGHEST
    )
    return cube_rows.reshape(count_rows, HA * HB) / math.sqrt(HA * HB)


def half_power(shift_vals):
    unit_scale = jnp.ones(shift_vals.shape, jnp.float32)
    factor = 0.5
    for bit_level in range(5):
        chosen = jnp.bitwise_and(jnp.right_shift(shift_vals, bit_level), 1) == 1
        unit_scale = unit_scale * jnp.where(chosen, factor, 1.0).astype(jnp.float32)
        factor = factor * factor
    return unit_scale


def butterfly(blocks):
    blocks = list(blocks)
    span = 1
    while span < len(blocks):
        for start in range(0, len(blocks), 2 * span):
            for j in range(start, start + span):
                u, v = blocks[j], blocks[j + span]
                blocks[j], blocks[j + span] = u + v, u - v
        span *= 2
    return blocks


def exact_powers(shift_vals):
    up = jnp.ones(shift_vals.shape, jnp.float32)
    down = jnp.ones(shift_vals.shape, jnp.float32)
    factor = 2.0
    for bit_level in range(5):
        chosen = jnp.bitwise_and(jnp.right_shift(shift_vals, bit_level), 1) == 1
        up = up * jnp.where(chosen, factor, 1.0)
        down = down * jnp.where(chosen, 1.0 / factor, 1.0)
        factor = factor * factor
    return up, down


def walsh_constant(table_order):
    positions = np.arange(table_order)
    common_bits = np.bitwise_and(positions[:, None], positions[None, :])
    parity = np.zeros((table_order, table_order), np.int64)
    for bit_level in range(max(table_order.bit_length() - 1, 1)):
        parity = parity + np.right_shift(common_bits, bit_level) % 2
    return jnp.asarray((1 - 2 * (parity % 2)).astype(np.float32), dtype=jnp.bfloat16)


def code_rows(y_ref, sh_ref, o_ref, group_rows, first_row, g, carry):
    rows = pl.ds(pl.multiple_of(g * 8, 8), 8)
    dest = g // (group_rows // 8)
    within = (g % (group_rows // 8)) * 8
    blocks = butterfly([y_ref[rows, a * HB:(a + 1) * HB] for a in range(HA)])
    base = first_row(dest) + within
    row_ids = lax.broadcasted_iota(jnp.int32, (8, 1), 0)
    shift_col = jnp.zeros((8, 1), jnp.int32)
    for j in range(8):
        shift_col = jnp.where(row_ids == j, sh_ref[0, 0, base + j], shift_col)
    up, dn = exact_powers(shift_col)
    up = up * (1.0 / math.sqrt(HA * HB))
    dn = dn.astype(jnp.bfloat16)
    for a in range(HA):
        coded = jnp.clip(blocks[a] * up, -127.0, 127.0).astype(jnp.bfloat16)
        o_ref[rows, a * HB:(a + 1) * HB] = (coded * dn).astype(o_ref.dtype)
    return carry


def code_kernel(part, x_size, mx_ref, sh_ref, x_ref, sg_ref, w_ref, *refs):
    out_refs, y_ref = refs[:-1], refs[-1]
    step = pl.program_id(0)
    groups, group_rows, _ = x_ref.shape
    dest_rows = group_rows * PARTS
    first_dest = ((mx_ref[0] + step) % x_size) * groups
    first_row = lambda dest: (first_dest + dest) * dest_rows + part * group_rows
    for a in range(HA):
        cols = slice(a * HB, (a + 1) * HB)
        sign = (2 * sg_ref[:, cols] - 1).astype(jnp.float32).astype(jnp.bfloat16)
        lhs = (x_ref[:, :, cols] * sign).reshape(groups * group_rows, HB)
        y_ref[:, cols] = jnp.dot(lhs, w_ref[...], preferred_element_type=jnp.float32)
    for k, o_ref in enumerate(out_refs):

        @pl.when(step == k)
        def _(o_ref=o_ref):
            coder = functools.partial(code_rows, y_ref, sh_ref, o_ref, group_rows, first_row)
            lax.fori_loop(0, groups * group_rows // 8, coder, 0)


def decoded_terms(grad_groups, signs, walsh, shifts, part, x_size):
    dests, _, part_rows, width = grad_groups.shape
    per_x = dests // x_size
    my_x = jnp.reshape(lax.axis_index("wx"), (1,)).astype(jnp.int32)
    tile = lambda i, mx, sh: ((mx[0] + i) % x_size, part, 0, 0)
    whole = lambda i, mx, sh: (0, 0)
    out_rows = per_x * part_rows
    return pl.pallas_call(
        functools.partial(code_kernel, part, x_size),
        grid_spec=pltpu.PrefetchScalarGridSpec(
            num_scalar_prefetch=2,
            grid=(x_size,),
            in_specs=[
                pl.BlockSpec((per_x, None, part_rows, width), tile),
                pl.BlockSpec((1, width), whole),
                pl.BlockSpec((HB, HB), whole),
            ],
            out_specs=[pl.BlockSpec((out_rows, width), whole) for _ in range(x_size)],
            scratch_shapes=[pltpu.VMEM((out_rows, width), jnp.float32)],
        ),
        out_shape=[jax.ShapeDtypeStruct((out_rows, width), jnp.bfloat16) for _ in range(x_size)],
        cost_estimate=pl.CostEstimate(
            flops=2 * dests * part_rows * width * HB + 8 * dests * part_rows * width,
            transcendentals=0,
            bytes_accessed=dests * part_rows * width * 4,
        ),
    )(my_x, shifts, grad_groups, signs, walsh)


def update_kernel(workers, p0_ref, p1_ref, f_ref, s_ref, w_ref, sg_ref, h_ref, sl_ref, ct_ref,
                  nf_ref, ns_ref, nw_ref, ch_ref, sd_ref, y_ref):
    half = p0_ref.shape[0]
    rows_all = 2 * half
    for part, p_ref in enumerate((p0_ref, p1_ref)):
        rows = slice(part * half, (part + 1) * half)
        mean_grad = p_ref[...] * (1.0 / workers)
        new_first = first_keep * f_ref[rows, :] + first_take * mean_grad
        new_second = second_keep * s_ref[rows, :] + second_take * mean_grad * mean_grad
        nf_ref[rows, :] = new_first
        ns_ref[rows, :] = new_second
        sd_ref[rows, :] = new_first / first_fix / (jnp.sqrt(new_second / second_fix) + adam_eps)
    stacked = jnp.concatenate([sd_ref[:, a * HB:(a + 1) * HB] for a in range(HA)], axis=0)
    high = stacked.astype(jnp.bfloat16)
    rest = stacked - high.astype(jnp.float32)
    mid = rest.astype(jnp.bfloat16)
    low = (rest - mid.astype(jnp.float32)).astype(jnp.bfloat16)
    walsh = h_ref[...]
    y_ref[...] = (
        jnp.dot(high, walsh, preferred_element_type=jnp.float32)
        + jnp.dot(mid, walsh, preferred_element_type=jnp.float32)
        + jnp.dot(low, walsh, preferred_element_type=jnp.float32)
    )
    for g in range(rows_all // 8):
        blocks = butterfly([y_ref[a * rows_all + g * 8:a * rows_all + g * 8 + 8, :] for a in range(HA)])
        for a in range(HA):
            cols = slice(a * HB, (a + 1) * HB)
            sign = (2 * sg_ref[:, cols] - 1).astype(jnp.float32)
            step = blocks[a] * (1.0 / math.sqrt(HA * HB)) * sign
            updated = w_ref[g * 8:g * 8 + 8, cols] - learn_rate * step
            nw_ref[g * 8:g * 8 + 8, cols] = updated
    owners, slots_per_list, piece_width = ch_ref.shape
    for owner in range(owners):
        used = ct_ref[0, 0, owner]
        owner_cols = slice(owner * piece_width, (owner + 1) * piece_width)
        listed = []
        for slot in range(slots_per_list):
            piece = nw_ref[pl.ds(sl_ref[0, 0, owner, slot], 1), owner_cols]
            listed.append(jnp.where(slot < used, piece, 0.0))
        ch_ref[owner] = jnp.concatenate(listed, axis=0).astype(ch_ref.dtype)


def adam_update(pieces, first_rows, second_rows, weight_rows, signs, walsh, workers, slots, counts):
    rows, width = first_rows.shape
    owners, cap = slots.shape[2], slots.shape[3]
    f32 = jax.ShapeDtypeStruct((rows, width), jnp.float32)
    vmem = pl.BlockSpec(memory_space=pltpu.VMEM)
    smem = pl.BlockSpec(memory_space=pltpu.SMEM)
    return pl.pallas_call(
        functools.partial(update_kernel, workers),
        in_specs=[vmem] * 7 + [smem, smem],
        out_specs=[vmem] * 4,
        out_shape=[f32, f32, f32, jax.ShapeDtypeStruct((owners, cap, width // owners), jnp.bfloat16)],
        scratch_shapes=[pltpu.VMEM((rows, width), jnp.float32), pltpu.VMEM((rows * HA, HB), jnp.float32)],
        cost_estimate=pl.CostEstimate(
            flops=6 * rows * width * HB, transcendentals=rows * width, bytes_accessed=rows * width * 32
        ),
    )(pieces[0], pieces[1], first_rows, second_rows, weight_rows, signs, walsh, slots, counts)


def send_along_x(terms, x_size):
    arrived = [terms[0]]
    for step in range(1, x_size):
        pairs = [(i, (i + step) % x_size) for i in range(x_size)]
        arrived.append(lax.ppermute(terms[step], "wx", pairs))
    return arrived


def sum_arrived(arrived):
    partial = arrived[0].astype(jnp.float32)
    for piece in arrived[1:]:
        partial = partial + piece.astype(jnp.float32)
    return partial


def select_pieces(slab_view, slot_lists, used_counts):
    gathered = jnp.take_along_axis(slab_view, slot_lists[:, :, None], axis=1)
    live_slots = lax.broadcasted_iota(jnp.int32, slot_lists.shape, 1) < used_counts[:, None]
    return jnp.where(live_slots[:, :, None], gathered, jnp.zeros((), jnp.bfloat16))


def per_device(grads, signs, shifts, first, second, weights, slots, counts):
    sign_vec = (2 * signs[0] - 1).astype(jnp.float32)
    grad_rows = grads[0, 0]
    blocks = first.shape[1]
    walsh = walsh_constant(HB)
    x_size = lax.axis_size("wx")
    dests = x_size * lax.axis_size("wz")
    workers = dests
    part_rows = blocks // PARTS
    grad_groups = grad_rows.reshape(dests, PARTS, part_rows, grad_rows.shape[-1])
    pieces = []
    terms = decoded_terms(grad_groups, signs, walsh, shifts, 0, x_size)
    arrived = send_along_x(terms, x_size)
    for part in range(1, PARTS + 1):
        if part < PARTS:
            terms = decoded_terms(grad_groups, signs, walsh, shifts, part, x_size)
            arrived, terms = lax.optimization_barrier((arrived, terms))
        partial = sum_arrived(arrived)
        pieces.append(lax.psum_scatter(partial, "wz", scatter_dimension=0, tiled=True))
        if part < PARTS:
            arrived = send_along_x(terms, x_size)
    new_first, new_second, new_weights, chosen_pieces = adam_update(
        pieces, first[0], second[0], weights[0], signs, walsh, workers, slots, counts
    )
    arrived = lax.all_to_all(chosen_pieces, "tensor", split_axis=0, concat_axis=0, tiled=True)
    return (new_first[None], new_second[None], new_weights[None], arrived[None, None])


def solution(mesh):
    dp_size, tensor_size = mesh.devices.shape
    split_mesh = Mesh(
        mesh.devices.reshape(X_CHIPS, dp_size // X_CHIPS, tensor_size), WORKERS + ("tensor",)
    )
    return jax.shard_map(
        per_device,
        mesh=split_mesh,
        in_specs=(
            P(WORKERS, "tensor", None, None),
            P("tensor", None),
            P(WORKERS, "tensor", None),
            P("tensor", WORKERS, None),
            P("tensor", WORKERS, None),
            P("tensor", WORKERS, None),
            P(WORKERS, "tensor", None, None),
            P(WORKERS, "tensor", None),
        ),
        out_specs=(
            P("tensor", WORKERS, None),
            P("tensor", WORKERS, None),
            P("tensor", WORKERS, None),
            P(WORKERS, "tensor", None, None, None),
        ),
        check_vma=False,
    )
```

```python
import functools
import math

import jax
import numpy as np
import jax.numpy as jnp
from jax import lax
from jax.experimental import pallas as pl
from jax.experimental.pallas import tpu as pltpu
from jax.sharding import Mesh
from jax.sharding import PartitionSpec as P

HA = 32
HB = 128
ROW_TILE = 256
X_CHIPS = 4
PARTS = 2
WORKERS = ("wx", "wz")


first_keep = 0.9
first_take = 0.1
second_keep = 0.95
second_take = 0.05
first_fix = 1.0 - 0.9**10
second_fix = 1.0 - 0.95**10
adam_eps = 1e-08
learn_rate = 0.2


def walsh_table(table_order):
    positions = jnp.arange(table_order, dtype=jnp.int32)
    common_bits = jnp.bitwise_and(positions[:, None], positions[None, :])
    parity_sum = jnp.zeros((table_order, table_order), jnp.int32)
    for bit_level in range(max(table_order.bit_length() - 1, 1)):
        parity_sum = parity_sum + jnp.bitwise_and(jnp.right_shift(common_bits, bit_level), 1)
    return (1 - 2 * jnp.bitwise_and(parity_sum, 1)).astype(jnp.float32)


def rotate(flat_rows):
    count_rows = flat_rows.shape[0]
    cube_rows = flat_rows.reshape(count_rows, HA, HB)
    cube_rows = jnp.einsum(
        "rab,bc->rac", cube_rows, walsh_table(HB), precision=lax.Precision.HIGHEST
    )
    cube_rows = jnp.einsum(
        "ka,rac->rkc", walsh_table(HA), cube_rows, precision=lax.Precision.HIGHEST
    )
    return cube_rows.reshape(count_rows, HA * HB) / math.sqrt(HA * HB)


def half_power(shift_vals):
    unit_scale = jnp.ones(shift_vals.shape, jnp.float32)
    factor = 0.5
    for bit_level in range(5):
        chosen = jnp.bitwise_and(jnp.right_shift(shift_vals, bit_level), 1) == 1
        unit_scale = unit_scale * jnp.where(chosen, factor, 1.0).astype(jnp.float32)
        factor = factor * factor
    return unit_scale


def butterfly(blocks):
    blocks = list(blocks)
    span = 1
    while span < len(blocks):
        for start in range(0, len(blocks), 2 * span):
            for j in range(start, start + span):
                u, v = blocks[j], blocks[j + span]
                blocks[j], blocks[j + span] = u + v, u - v
        span *= 2
    return blocks


def exact_powers(shift_vals):
    up = jnp.ones(shift_vals.shape, jnp.float32)
    down = jnp.ones(shift_vals.shape, jnp.float32)
    factor = 2.0
    for bit_level in range(5):
        chosen = jnp.bitwise_and(jnp.right_shift(shift_vals, bit_level), 1) == 1
        up = up * jnp.where(chosen, factor, 1.0)
        down = down * jnp.where(chosen, 1.0 / factor, 1.0)
        factor = factor * factor
    return up, down


def walsh_constant(table_order):
    positions = np.arange(table_order)
    common_bits = np.bitwise_and(positions[:, None], positions[None, :])
    parity = np.zeros((table_order, table_order), np.int64)
    for bit_level in range(max(table_order.bit_length() - 1, 1)):
        parity = parity + np.right_shift(common_bits, bit_level) % 2
    return jnp.asarray((1 - 2 * (parity % 2)).astype(np.float32), dtype=jnp.bfloat16)


def code_rows(y_ref, sh_ref, o_ref, group_rows, first_row, g, carry):
    rows = pl.ds(pl.multiple_of(g * 8, 8), 8)
    dest = g // (group_rows // 8)
    within = (g % (group_rows // 8)) * 8
    blocks = butterfly([y_ref[rows, a * HB:(a + 1) * HB] for a in range(HA)])
    base = first_row(dest) + within
    row_ids = lax.broadcasted_iota(jnp.int32, (8, 1), 0)
    shift_col = jnp.zeros((8, 1), jnp.int32)
    for j in range(8):
        shift_col = jnp.where(row_ids == j, sh_ref[0, 0, base + j], shift_col)
    up, dn = exact_powers(shift_col)
    up = up * (1.0 / math.sqrt(HA * HB))
    dn = dn.astype(jnp.bfloat16)
    for a in range(HA):
        coded = jnp.clip(blocks[a] * up, -127.0, 127.0).astype(jnp.bfloat16)
        o_ref[rows, a * HB:(a + 1) * HB] = (coded * dn).astype(o_ref.dtype)
    return carry


def code_kernel(part, x_size, mx_ref, sh_ref, x_ref, sg_ref, w_ref, *refs):
    out_refs, y_ref = refs[:-1], refs[-1]
    step = pl.program_id(0)
    groups, group_rows, _ = x_ref.shape
    dest_rows = group_rows * PARTS
    first_dest = ((mx_ref[0] + step) % x_size) * groups
    first_row = lambda dest: (first_dest + dest) * dest_rows + part * group_rows
    for a in range(HA):
        cols = slice(a * HB, (a + 1) * HB)
        sign = (2 * sg_ref[:, cols] - 1).astype(jnp.float32).astype(jnp.bfloat16)
        lhs = (x_ref[:, :, cols] * sign).reshape(groups * group_rows, HB)
        y_ref[:, cols] = jnp.dot(lhs, w_ref[...], preferred_element_type=jnp.float32)
    for k, o_ref in enumerate(out_refs):

        @pl.when(step == k)
        def _(o_ref=o_ref):
            coder = functools.partial(code_rows, y_ref, sh_ref, o_ref, group_rows, first_row)
            lax.fori_loop(0, groups * group_rows // 8, coder, 0)


def decoded_terms(grad_groups, signs, walsh, shifts, part, x_size):
    dests, _, part_rows, width = grad_groups.shape
    per_x = dests // x_size
    my_x = jnp.reshape(lax.axis_index("wx"), (1,)).astype(jnp.int32)
    tile = lambda i, mx, sh: ((mx[0] + i) % x_size, part, 0, 0)
    whole = lambda i, mx, sh: (0, 0)
    out_rows = per_x * part_rows
    return pl.pallas_call(
        functools.partial(code_kernel, part, x_size),
        grid_spec=pltpu.PrefetchScalarGridSpec(
            num_scalar_prefetch=2,
            grid=(x_size,),
            in_specs=[
                pl.BlockSpec((per_x, None, part_rows, width), tile),
                pl.BlockSpec((1, width), whole),
                pl.BlockSpec((HB, HB), whole),
            ],
            out_specs=[pl.BlockSpec((out_rows, width), whole) for _ in range(x_size)],
            scratch_shapes=[pltpu.VMEM((out_rows, width), jnp.float32)],
        ),
        out_shape=[jax.ShapeDtypeStruct((out_rows, width), jnp.bfloat16) for _ in range(x_size)],
        cost_estimate=pl.CostEstimate(
            flops=2 * dests * part_rows * width * HB + 8 * dests * part_rows * width,
            transcendentals=0,
            bytes_accessed=dests * part_rows * width * 4,
        ),
    )(my_x, shifts, grad_groups, signs, walsh)


def update_kernel(workers, p0_ref, p1_ref, f_ref, s_ref, w_ref, sg_ref, h_ref, sl_ref, ct_ref,
                  nf_ref, ns_ref, nw_ref, ch_ref, sd_ref, y_ref):
    half = p0_ref.shape[0]
    rows_all = 2 * half
    for part, p_ref in enumerate((p0_ref, p1_ref)):
        rows = slice(part * half, (part + 1) * half)
        mean_grad = p_ref[...] * (1.0 / workers)
        new_first = first_keep * f_ref[rows, :] + first_take * mean_grad
        new_second = second_keep * s_ref[rows, :] + second_take * mean_grad * mean_grad
        nf_ref[rows, :] = new_first
        ns_ref[rows, :] = new_second
        sd_ref[rows, :] = new_first / first_fix / (jnp.sqrt(new_second / second_fix) + adam_eps)
    stacked = jnp.concatenate([sd_ref[:, a * HB:(a + 1) * HB] for a in range(HA)], axis=0)
    high = stacked.astype(jnp.bfloat16)
    rest = stacked - high.astype(jnp.float32)
    mid = rest.astype(jnp.bfloat16)
    low = (rest - mid.astype(jnp.float32)).astype(jnp.bfloat16)
    walsh = h_ref[...]
    y_ref[...] = (
        jnp.dot(high, walsh, preferred_element_type=jnp.float32)
        + jnp.dot(mid, walsh, preferred_element_type=jnp.float32)
        + jnp.dot(low, walsh, preferred_element_type=jnp.float32)
    )
    for g in range(rows_all // 8):
        blocks = butterfly([y_ref[a * rows_all + g * 8:a * rows_all + g * 8 + 8, :] for a in range(HA)])
        for a in range(HA):
            cols = slice(a * HB, (a + 1) * HB)
            sign = (2 * sg_ref[:, cols] - 1).astype(jnp.float32)
            step = blocks[a] * (1.0 / math.sqrt(HA * HB)) * sign
            updated = w_ref[g * 8:g * 8 + 8, cols] - learn_rate * step
            nw_ref[g * 8:g * 8 + 8, cols] = updated
    owners, slots_per_list, piece_width = ch_ref.shape
    for owner in range(owners):
        used = ct_ref[0, 0, owner]
        owner_cols = slice(owner * piece_width, (owner + 1) * piece_width)
        listed = []
        for slot in range(slots_per_list):
            piece = nw_ref[pl.ds(sl_ref[0, 0, owner, slot], 1), owner_cols]
            listed.append(jnp.where(slot < used, piece, 0.0))
        ch_ref[owner] = jnp.concatenate(listed, axis=0).astype(ch_ref.dtype)


def adam_update(pieces, first_rows, second_rows, weight_rows, signs, walsh, workers, slots, counts):
    rows, width = first_rows.shape
    owners, cap = slots.shape[2], slots.shape[3]
    f32 = jax.ShapeDtypeStruct((rows, width), jnp.float32)
    vmem = pl.BlockSpec(memory_space=pltpu.VMEM)
    smem = pl.BlockSpec(memory_space=pltpu.SMEM)
    return pl.pallas_call(
        functools.partial(update_kernel, workers),
        in_specs=[vmem] * 7 + [smem, smem],
        out_specs=[vmem] * 4,
        out_shape=[f32, f32, f32, jax.ShapeDtypeStruct((owners, cap, width // owners), jnp.bfloat16)],
        scratch_shapes=[pltpu.VMEM((rows, width), jnp.float32), pltpu.VMEM((rows * HA, HB), jnp.float32)],
        cost_estimate=pl.CostEstimate(
            flops=6 * rows * width * HB, transcendentals=rows * width, bytes_accessed=rows * width * 32
        ),
    )(pieces[0], pieces[1], first_rows, second_rows, weight_rows, signs, walsh, slots, counts)


def send_along_x(terms, x_size):
    far = x_size // 2
    arrived = [terms[0]]
    for step in [far] + [k for k in range(1, x_size) if k != far]:
        pairs = [(i, (i + step) % x_size) for i in range(x_size)]
        arrived.append(lax.ppermute(terms[step], "wx", pairs))
    return arrived


def sum_arrived(arrived):
    partial = arrived[0].astype(jnp.float32)
    for piece in arrived[1:]:
        partial = partial + piece.astype(jnp.float32)
    return partial


def select_pieces(slab_view, slot_lists, used_counts):
    gathered = jnp.take_along_axis(slab_view, slot_lists[:, :, None], axis=1)
    live_slots = lax.broadcasted_iota(jnp.int32, slot_lists.shape, 1) < used_counts[:, None]
    return jnp.where(live_slots[:, :, None], gathered, jnp.zeros((), jnp.bfloat16))


def per_device(grads, signs, shifts, first, second, weights, slots, counts):
    sign_vec = (2 * signs[0] - 1).astype(jnp.float32)
    grad_rows = grads[0, 0]
    blocks = first.shape[1]
    walsh = walsh_constant(HB)
    x_size = lax.axis_size("wx")
    dests = x_size * lax.axis_size("wz")
    workers = dests
    part_rows = blocks // PARTS
    grad_groups = grad_rows.reshape(dests, PARTS, part_rows, grad_rows.shape[-1])
    pieces = []
    terms = decoded_terms(grad_groups, signs, walsh, shifts, 0, x_size)
    arrived = send_along_x(terms, x_size)
    for part in range(1, PARTS + 1):
        if part < PARTS:
            terms = decoded_terms(grad_groups, signs, walsh, shifts, part, x_size)
            arrived, terms = lax.optimization_barrier((arrived, terms))
        partial = sum_arrived(arrived)
        pieces.append(lax.psum_scatter(partial, "wz", scatter_dimension=0, tiled=True))
        if part < PARTS:
            arrived = send_along_x(terms, x_size)
    new_first, new_second, new_weights, chosen_pieces = adam_update(
        pieces, first[0], second[0], weights[0], signs, walsh, workers, slots, counts
    )
    arrived = lax.all_to_all(chosen_pieces, "tensor", split_axis=0, concat_axis=0, tiled=True)
    return (new_first[None], new_second[None], new_weights[None], arrived[None, None])


def solution(mesh):
    dp_size, tensor_size = mesh.devices.shape
    split_mesh = Mesh(
        mesh.devices.reshape(X_CHIPS, dp_size // X_CHIPS, tensor_size), WORKERS + ("tensor",)
    )
    return jax.shard_map(
        per_device,
        mesh=split_mesh,
        in_specs=(
            P(WORKERS, "tensor", None, None),
            P("tensor", None),
            P(WORKERS, "tensor", None),
            P("tensor", WORKERS, None),
            P("tensor", WORKERS, None),
            P("tensor", WORKERS, None),
            P(WORKERS, "tensor", None, None),
            P(WORKERS, "tensor", None),
        ),
        out_specs=(
            P("tensor", WORKERS, None),
            P("tensor", WORKERS, None),
            P("tensor", WORKERS, None),
            P(WORKERS, "tensor", None, None, None),
        ),
        check_vma=False,
    )
```
